512 devices in a mesh: feat: 16 (over x, z_hi, core), samp: 32 (over y, z_lo).
Axes of the slice: x: 4, y: 8, z: 8 (z_hi: 2, z_lo: 4; z = z_hi * 4 + z_lo), core: 2. Of those that a mesh axis runs over, the one named last changes fastest.
Arguments:
- tier_one: bfloat16 [8192, 12288], P('feat', 'samp')
- residuals: bfloat16 [12288, 128], P('samp'), may hold values from -6 to 6
- pair_list: int32 [3, 65536], P(None, 'feat'), may hold values from 0 to 8191, as said below
Outputs:
- scores: float32 [65536, 128], P(('feat', 'samp'))
The draws below stay inside these ranges and needn't reach their ends.
Inputs may be any that keep to these rules, and one draw needn't show every extreme that they name: `pair_list`: rows 0 and 1 are feature indices, row 2 an operator id of 0 to 3; each descriptor's two features differ.
All inputs are finite; a program needn't handle non-finite values.
Results may differ from the reference program's by a relative error of at most 0.0031.
Values may be sent and summed in bfloat16 or wider, within the bound.
No kernel may reach another device: no remote copies, remote signals or barrier semaphores. Data moves between devices by JAX's collectives and lax.ppermute only.
A program may use at most 64 MiB of HBM per device.

```python
import math
import jax
import jax.numpy as jnp
from jax import lax

F1 = 8192
K = 128
P_SIZE = 65536
SAMPLES = 12288


def draw_tier_one(key, part):
    keys = jax.random.split(key, 4)
    sample_pos = jnp.arange(SAMPLES, dtype=jnp.float32)
    rising = 1.0 + 2.0 * sample_pos / max(SAMPLES - 1, 1)
    feat_scale = jnp.exp(jax.random.uniform(keys[0], (F1, 1), jnp.float32, math.log(0.3), math.log(3.0)))
    feat_mean = jax.random.uniform(keys[1], (F1, 1), jnp.float32, -1.0, 1.0)
    roughness = jnp.exp(jax.random.uniform(keys[2], (1, SAMPLES), jnp.float32, math.log(0.5), math.log(2.0)))
    noise_part = jnp.clip(jax.random.normal(keys[3], (F1, SAMPLES), jnp.float32), -4.0, 4.0)
    return (feat_mean + feat_scale * rising[None, :] * roughness * noise_part).astype(jnp.bfloat16)


def draw_pair_list(key, part):
    keys = jax.random.split(jax.random.fold_in(key, 7), 3)
    first_idx = jax.random.randint(keys[0], (P_SIZE,), 0, F1, jnp.int32)
    offset = jax.random.randint(keys[1], (P_SIZE,), 1, F1, jnp.int32)
    second_idx = (first_idx + offset) % F1
    operator_id = jax.random.randint(keys[2], (P_SIZE,), 0, 4, jnp.int32)
    return jnp.stack([first_idx, second_idx, operator_id], axis=0).astype(jnp.int32)


def block_levels(rng, dims, pieces, smallest, top_value):
    factor_of = 1.0
    for position, blocks in pieces:
        heights = jax.random.uniform(jax.random.fold_in(jax.random.fold_in(rng, 6), position), (blocks,), jnp.float32, smallest / len(pieces), top_value / len(pieces))
        factor_of = factor_of * jnp.repeat(jnp.exp(heights), dims[position] // blocks).reshape((-1,) + (1,) * (len(dims) - 1 - position))
    return factor_of


def bell_draw(own_key, dims, width, reach, cuts=(), held_as=jnp.bfloat16):
    entries = jax.random.normal(own_key, dims, jnp.float32) * width
    if len(cuts) > 0:
        entries = block_levels(own_key, dims, cuts, -0.22, 0.18) * entries
    return jnp.clip(entries, min=-reach, max=reach).astype(held_as)


def setup_inputs(seed: int = 0) -> dict:
    seeds = jax.random.split(jax.random.key(seed), 4)
    tier_one = draw_tier_one(jax.random.fold_in(seeds[3], 71), 0)
    residuals = bell_draw(seeds[1], (SAMPLES, K), 1.0, 6.0, ((0, 32),))
    pair_list = draw_pair_list(jax.random.fold_in(seeds[3], 71), 0)
    return dict(tier_one=tier_one, residuals=residuals, pair_list=pair_list)


epsilon = 1e-05

def descriptors(tier_one, pair_cols):
    first_rows = jnp.take(tier_one, pair_cols[0], axis=0).astype(jnp.float32)
    second_rows = jnp.take(tier_one, pair_cols[1], axis=0).astype(jnp.float32)
    operator_id = pair_cols[2][:, None]
    quotient = first_rows / (1.0 + jnp.abs(second_rows))
    built = jnp.where(operator_id == 0, first_rows + second_rows, jnp.where(operator_id == 1, first_rows - second_rows, jnp.where(operator_id == 2, first_rows * second_rows, quotient)))
    return built.astype(jnp.bfloat16)

def block_terms(tier_one, residuals, pair_cols):
    built = descriptors(tier_one, pair_cols)
    product = jnp.dot(built, residuals, preferred_element_type=jnp.float32)
    widened = built.astype(jnp.float32)
    return (product, lax.optimization_barrier(jnp.sum(widened, axis=1)), lax.optimization_barrier(jnp.sum(widened * widened, axis=1)))

def finish(product, first_sums, square_sums, col_totals, sample_count):
    means = first_sums / sample_count
    variance = square_sums / sample_count - means * means
    centred = product - means[:, None] * col_totals[None, :]
    return centred * lax.rsqrt(variance + epsilon)[:, None] / math.sqrt(sample_count)

def reference(tier_one, residuals, pair_list):
    block_size = math.gcd(P_SIZE, 1024)
    block_count = P_SIZE // block_size
    grouped = pair_list.reshape(3, block_count, block_size).transpose(1, 0, 2)
    product, first_sums, square_sums = lax.map(lambda pair_cols: block_terms(tier_one, residuals, pair_cols), grouped)
    product = product.reshape(P_SIZE, K)
    first_sums = first_sums.reshape(P_SIZE)
    square_sums = square_sums.reshape(P_SIZE)
    col_totals = lax.optimization_barrier(jnp.sum(residuals.astype(jnp.float32), axis=0))
    return finish(product, first_sums, square_sums, col_totals, SAMPLES)
```

```python
import math

import jax
import jax.numpy as jnp
import numpy as np
from jax import lax
from jax.sharding import Mesh
from jax.sharding import PartitionSpec as P

epsilon = 1e-05

FEAT_AXES = ("x", "zh", "c")
SAMP_AXES = ("y", "zl")
EXTRA_ROWS = 8


def combine_rows(first_rows, second_rows, operator_id):
    first_rows = first_rows.astype(jnp.float32)
    second_rows = second_rows.astype(jnp.float32)
    quotient = first_rows / (1.0 + jnp.abs(second_rows))
    built = jnp.where(
        operator_id == 0,
        first_rows + second_rows,
        jnp.where(
            operator_id == 1,
            first_rows - second_rows,
            jnp.where(operator_id == 2, first_rows * second_rows, quotient),
        ),
    )
    return built.astype(jnp.bfloat16)


def finish(product, first_sums, square_sums, col_totals, sample_count):
    means = first_sums / sample_count
    variance = square_sums / sample_count - means * means
    centred = product - means[:, None] * col_totals[None, :]
    return centred * lax.rsqrt(variance + epsilon)[:, None] / math.sqrt(sample_count)


def per_device(tier_one, residuals, pair_list):
    local_rows = tier_one.shape[0]
    local_pairs = pair_list.shape[1]
    width_k = residuals.shape[1]
    n_x = lax.axis_size("x")
    n_zh = lax.axis_size("zh")
    n_y = lax.axis_size("y")
    n_zl = lax.axis_size("zl")
    n_samp = n_y * n_zl
    sample_count = residuals.shape[0] * n_samp

    rows = lax.all_gather(tier_one, "zh", axis=0, tiled=True)
    rows = lax.all_gather(rows, "x", axis=0, tiled=True)
    rows = lax.all_gather(rows, "c", axis=0, tiled=True)

    def position(g):
        f, r = g // local_rows, g % local_rows
        x, zh, c = f // (2 * n_zh), (f // 2) % n_zh, f % 2
        return ((c * n_x + x) * n_zh + zh) * local_rows + r

    first = jnp.take(rows, position(pair_list[0]), axis=0)
    second = jnp.take(rows, position(pair_list[1]), axis=0)
    built = combine_rows(first, second, pair_list[2][:, None])

    product = jnp.dot(built, residuals, preferred_element_type=jnp.float32)
    widened = built.astype(jnp.float32)
    first_sums = jnp.sum(widened, axis=1)
    square_sums = jnp.sum(widened * widened, axis=1)
    col_part = jnp.sum(residuals.astype(jnp.float32), axis=0)

    blocks = local_pairs // width_k
    block_rows = width_k + EXTRA_ROWS
    packed = jnp.concatenate(
        [
            product.reshape(blocks, width_k, width_k),
            jnp.broadcast_to(col_part[None, None, :], (blocks, 1, width_k)),
            first_sums.reshape(blocks, 1, width_k),
            square_sums.reshape(blocks, 1, width_k),
            jnp.zeros((blocks, EXTRA_ROWS - 3, width_k), jnp.float32),
        ],
        axis=1,
    ).reshape(blocks * block_rows, width_k)
    owned = lax.psum_scatter(packed, "y", scatter_dimension=0, tiled=True)
    owned = lax.psum_scatter(owned, "zl", scatter_dimension=0, tiled=True)

    return finish(
        owned[:width_k], owned[width_k + 1], owned[width_k + 2], owned[width_k],
        sample_count,
    )


def solution(mesh):
    n_feat, n_samp = mesh.devices.shape
    n_c, n_zh = 2, 2
    n_x = n_feat // (n_c * n_zh)
    n_zl = 4
    n_y = n_samp // n_zl
    devices = np.asarray(mesh.devices).reshape(n_x, n_zh, n_c, n_y, n_zl)
    fine = Mesh(devices, FEAT_AXES + SAMP_AXES)
    in_specs = (P(FEAT_AXES, SAMP_AXES), P(SAMP_AXES, None), P(None, FEAT_AXES))
    out_specs = P(FEAT_AXES + SAMP_AXES, None)
    return jax.shard_map(
        per_device, mesh=fine, in_specs=in_specs, out_specs=out_specs, check_vma=False
    )
```

```python
import math

import jax
import jax.numpy as jnp
import numpy as np
from jax import lax
from jax.sharding import Mesh
from jax.sharding import PartitionSpec as P

epsilon = 1e-05

FEAT_AXES = ("x", "zh", "c")
SAMP_AXES = ("y", "zl")
EXTRA_ROWS = 8


def combine_rows(first_rows, second_rows, operator_id):
    first_rows = first_rows.astype(jnp.float32)
    second_rows = second_rows.astype(jnp.float32)
    quotient = first_rows / (1.0 + jnp.abs(second_rows))
    built = jnp.where(
        operator_id == 0,
        first_rows + second_rows,
        jnp.where(
            operator_id == 1,
            first_rows - second_rows,
            jnp.where(operator_id == 2, first_rows * second_rows, quotient),
        ),
    )
    return built.astype(jnp.bfloat16)


def finish(product, first_sums, square_sums, col_totals, sample_count):
    means = first_sums / sample_count
    variance = square_sums / sample_count - means * means
    centred = product - means[:, None] * col_totals[None, :]
    return centred * lax.rsqrt(variance + epsilon)[:, None] / math.sqrt(sample_count)


def per_device(tier_one, residuals, pair_list):
    local_rows = tier_one.shape[0]
    local_pairs = pair_list.shape[1]
    width_k = residuals.shape[1]
    n_x = lax.axis_size("x")
    n_zh = lax.axis_size("zh")
    n_y = lax.axis_size("y")
    n_zl = lax.axis_size("zl")
    n_samp = n_y * n_zl
    sample_count = residuals.shape[0] * n_samp

    rows = lax.all_gather(tier_one, "zh", axis=0, tiled=True)
    rows = lax.all_gather(rows, "x", axis=0, tiled=True)
    other = lax.ppermute(rows, "c", perm=[(0, 1), (1, 0)])
    rows = jnp.concatenate([rows, other], axis=0)
    my_c = lax.axis_index("c")

    def position(g):
        f, r = g // local_rows, g % local_rows
        x, zh, c = f // (2 * n_zh), (f // 2) % n_zh, f % 2
        half = (c != my_c).astype(jnp.int32)
        return ((half * n_x + x) * n_zh + zh) * local_rows + r

    first = jnp.take(rows, position(pair_list[0]), axis=0)
    second = jnp.take(rows, position(pair_list[1]), axis=0)
    built = combine_rows(first, second, pair_list[2][:, None])

    product = jnp.dot(built, residuals, preferred_element_type=jnp.float32)
    widened = built.astype(jnp.float32)
    first_sums = jnp.sum(widened, axis=1)
    square_sums = jnp.sum(widened * widened, axis=1)
    col_part = jnp.sum(residuals.astype(jnp.float32), axis=0)

    blocks = local_pairs // width_k
    block_rows = width_k + EXTRA_ROWS
    packed = jnp.concatenate(
        [
            product.reshape(blocks, width_k, width_k),
            jnp.broadcast_to(col_part[None, None, :], (blocks, 1, width_k)),
            first_sums.reshape(blocks, 1, width_k),
            square_sums.reshape(blocks, 1, width_k),
            jnp.zeros((blocks, EXTRA_ROWS - 3, width_k), jnp.float32),
        ],
        axis=1,
    ).reshape(blocks * block_rows, width_k)
    owned = lax.psum_scatter(packed, "y", scatter_dimension=0, tiled=True)
    my_zl = lax.axis_index("zl")
    total = lax.dynamic_slice_in_dim(owned, my_zl * block_rows, block_rows, 0)
    for shift in range(1, n_zl):
        dest = (my_zl + shift) % n_zl
        piece = lax.dynamic_slice_in_dim(owned, dest * block_rows, block_rows, 0)
        total = total + lax.ppermute(
            piece, "zl", perm=[(i, (i + shift) % n_zl) for i in range(n_zl)]
        )
    owned = total

    return finish(
        owned[:width_k], owned[width_k + 1], owned[width_k + 2], owned[width_k],
        sample_count,
    )


def solution(mesh):
    n_feat, n_samp = mesh.devices.shape
    n_c, n_zh = 2, 2
    n_x = n_feat // (n_c * n_zh)
    n_zl = 4
    n_y = n_samp // n_zl
    devices = np.asarray(mesh.devices).reshape(n_x, n_zh, n_c, n_y, n_zl)
    fine = Mesh(devices, FEAT_AXES + SAMP_AXES)
    in_specs = (P(FEAT_AXES, SAMP_AXES), P(SAMP_AXES, None), P(None, FEAT_AXES))
    out_specs = P(FEAT_AXES + SAMP_AXES, None)
    return jax.shard_map(
        per_device, mesh=fine, in_specs=in_specs, out_specs=out_specs, check_vma=False
    )
```

```python
import math

import jax
import jax.numpy as jnp
import numpy as np
from jax import lax
from jax.sharding import Mesh
from jax.sharding import PartitionSpec as P

epsilon = 1e-05

FEAT_AXES = ("x", "zh", "c")
SAMP_AXES = ("y", "zl")
EXTRA_ROWS = 8


def combine_rows(first_rows, second_rows, operator_id):
    first_rows = first_rows.astype(jnp.float32)
    second_rows = second_rows.astype(jnp.float32)
    quotient = first_rows / (1.0 + jnp.abs(second_rows))
    built = jnp.where(
        operator_id == 0,
        first_rows + second_rows,
        jnp.where(
            operator_id == 1,
            first_rows - second_rows,
            jnp.where(operator_id == 2, first_rows * second_rows, quotient),
        ),
    )
    return built.astype(jnp.bfloat16)


def finish(product, first_sums, square_sums, col_totals, sample_count):
    means = first_sums / sample_count
    variance = square_sums / sample_count - means * means
    centred = product - means[:, None] * col_totals[None, :]
    return centred * lax.rsqrt(variance + epsilon)[:, None] / math.sqrt(sample_count)


def per_device(tier_one, residuals, pair_list):
    local_rows = tier_one.shape[0]
    local_pairs = pair_list.shape[1]
    width_k = residuals.shape[1]
    n_x = lax.axis_size("x")
    n_zh = lax.axis_size("zh")
    n_y = lax.axis_size("y")
    n_zl = lax.axis_size("zl")
    n_samp = n_y * n_zl
    sample_count = residuals.shape[0] * n_samp

    my_zh = lax.axis_index("zh")
    my_c = lax.axis_index("c")

    def position(g):
        f, r = g // local_rows, g % local_rows
        x, zh, c = f // (2 * n_zh), (f // 2) % n_zh, f % 2
        c_half = (c != my_c).astype(jnp.int32)
        zh_half = (zh != my_zh).astype(jnp.int32)
        return ((c_half * n_x + x) * n_zh + zh_half) * local_rows + r

    first_pos = position(pair_list[0])
    second_pos = position(pair_list[1])
    operator_id = pair_list[2][:, None]

    local_samples = tier_one.shape[1]
    chunk = 128 if local_samples % 128 == 0 else local_samples
    product = first_sums = square_sums = None
    for start in range(0, local_samples, chunk):
        part = tier_one[:, start:start + chunk]
        part = jnp.concatenate(
            [part, lax.ppermute(part, "zh", perm=[(0, 1), (1, 0)])], axis=0
        )
        part = lax.all_gather(part, "x", axis=0, tiled=True)
        part = jnp.concatenate(
            [part, lax.ppermute(part, "c", perm=[(0, 1), (1, 0)])], axis=0
        )
        first = jnp.take(part, first_pos, axis=0)
        second = jnp.take(part, second_pos, axis=0)
        built = combine_rows(first, second, operator_id)
        res_part = residuals[start:start + chunk]
        step_product = jnp.dot(built, res_part, preferred_element_type=jnp.float32)
        widened = built.astype(jnp.float32)
        step_first = jnp.sum(widened, axis=1)
        step_square = jnp.sum(widened * widened, axis=1)
        if product is None:
            product, first_sums, square_sums = step_product, step_first, step_square
        else:
            product = product + step_product
            first_sums = first_sums + step_first
            square_sums = square_sums + step_square
    col_part = jnp.sum(residuals.astype(jnp.float32), axis=0)

    blocks = local_pairs // width_k
    block_rows = width_k + EXTRA_ROWS
    packed = jnp.concatenate(
        [
            product.reshape(blocks, width_k, width_k),
            jnp.broadcast_to(col_part[None, None, :], (blocks, 1, width_k)),
            first_sums.reshape(blocks, 1, width_k),
            square_sums.reshape(blocks, 1, width_k),
            jnp.zeros((blocks, EXTRA_ROWS - 3, width_k), jnp.float32),
        ],
        axis=1,
    ).reshape(blocks * block_rows, width_k)
    owned = lax.psum_scatter(packed, "y", scatter_dimension=0, tiled=True)
    my_zl = lax.axis_index("zl")
    total = lax.dynamic_slice_in_dim(owned, my_zl * block_rows, block_rows, 0)
    for shift in range(1, n_zl):
        dest = (my_zl + shift) % n_zl
        piece = lax.dynamic_slice_in_dim(owned, dest * block_rows, block_rows, 0)
        total = total + lax.ppermute(
            piece, "zl", perm=[(i, (i + shift) % n_zl) for i in range(n_zl)]
        )
    owned = total

    return finish(
        owned[:width_k], owned[width_k + 1], owned[width_k + 2], owned[width_k],
        sample_count,
    )


def solution(mesh):
    n_feat, n_samp = mesh.devices.shape
    n_c, n_zh = 2, 2
    n_x = n_feat // (n_c * n_zh)
    n_zl = 4
    n_y = n_samp // n_zl
    devices = np.asarray(mesh.devices).reshape(n_x, n_zh, n_c, n_y, n_zl)
    fine = Mesh(devices, FEAT_AXES + SAMP_AXES)
    in_specs = (P(FEAT_AXES, SAMP_AXES), P(SAMP_AXES, None), P(None, FEAT_AXES))
    out_specs = P(FEAT_AXES + SAMP_AXES, None)
    return jax.shard_map(
        per_device, mesh=fine, in_specs=in_specs, out_specs=out_specs, check_vma=False
    )
```

```python
import math

import jax
import jax.numpy as jnp
import numpy as np
from jax import lax
from jax.sharding import Mesh
from jax.sharding import PartitionSpec as P

epsilon = 1e-05

FEAT_AXES = ("x", "zh", "c")
SAMP_AXES = ("y", "zl")
EXTRA_ROWS = 8


def combine_rows(first_rows, second_rows, operator_id):
    first_rows = first_rows.astype(jnp.float32)
    second_rows = second_rows.astype(jnp.float32)
    quotient = first_rows / (1.0 + jnp.abs(second_rows))
    built = jnp.where(
        operator_id == 0,
        first_rows + second_rows,
        jnp.where(
            operator_id == 1,
            first_rows - second_rows,
            jnp.where(operator_id == 2, first_rows * second_rows, quotient),
        ),
    )
    return built.astype(jnp.bfloat16)


def ring_gather(block, axis, n):
    assert n == 4
    fwd = [(i, (i + 1) % n) for i in range(n)]
    bwd = [(i, (i - 1) % n) for i in range(n)]
    from_left = lax.ppermute(block, axis, perm=fwd)
    from_right = lax.ppermute(block, axis, perm=bwd)
    half = block.shape[0] // 2
    far_a = lax.ppermute(from_left[:half], axis, perm=fwd)
    far_b = lax.ppermute(from_right[half:], axis, perm=bwd)
    return jnp.concatenate([block, from_right, far_a, far_b, from_left], axis=0)


def finish(product, first_sums, square_sums, col_totals, sample_count):
    means = first_sums / sample_count
    variance = square_sums / sample_count - means * means
    centred = product - means[:, None] * col_totals[None, :]
    return centred * lax.rsqrt(variance + epsilon)[:, None] / math.sqrt(sample_count)


def per_device(tier_one, residuals, pair_list):
    local_rows = tier_one.shape[0]
    local_pairs = pair_list.shape[1]
    width_k = residuals.shape[1]
    n_x = lax.axis_size("x")
    n_zh = lax.axis_size("zh")
    n_y = lax.axis_size("y")
    n_zl = lax.axis_size("zl")
    n_samp = n_y * n_zl
    sample_count = residuals.shape[0] * n_samp

    rows = lax.all_gather(tier_one, "zh", axis=0, tiled=True)
    rows = ring_gather(rows, "x", n_x)
    other = lax.ppermute(rows, "c", perm=[(0, 1), (1, 0)])
    rows = jnp.concatenate([rows, other], axis=0)
    my_c = lax.axis_index("c")
    my_x = lax.axis_index("x")

    def position(g):
        f, r = g // local_rows, g % local_rows
        x, zh, c = f // (2 * n_zh), (f // 2) % n_zh, f % 2
        half = (c != my_c).astype(jnp.int32)
        x_slot = (x - my_x + n_x) % n_x
        return ((half * n_x + x_slot) * n_zh + zh) * local_rows + r

    first = jnp.take(rows, position(pair_list[0]), axis=0)
    second = jnp.take(rows, position(pair_list[1]), axis=0)
    built = combine_rows(first, second, pair_list[2][:, None])

    product = jnp.dot(built, residuals, preferred_element_type=jnp.float32)
    widened = built.astype(jnp.float32)
    first_sums = jnp.sum(widened, axis=1)
    square_sums = jnp.sum(widened * widened, axis=1)
    col_part = jnp.sum(residuals.astype(jnp.float32), axis=0)

    blocks = local_pairs // width_k
    block_rows = width_k + EXTRA_ROWS
    packed = jnp.concatenate(
        [
            product.reshape(blocks, width_k, width_k),
            jnp.broadcast_to(col_part[None, None, :], (blocks, 1, width_k)),
            first_sums.reshape(blocks, 1, width_k),
            square_sums.reshape(blocks, 1, width_k),
            jnp.zeros((blocks, EXTRA_ROWS - 3, width_k), jnp.float32),
        ],
        axis=1,
    ).reshape(blocks * block_rows, width_k)
    owned = lax.psum_scatter(packed, "y", scatter_dimension=0, tiled=True)
    my_zl = lax.axis_index("zl")
    total = lax.dynamic_slice_in_dim(owned, my_zl * block_rows, block_rows, 0)
    for shift in range(1, n_zl):
        dest = (my_zl + shift) % n_zl
        piece = lax.dynamic_slice_in_dim(owned, dest * block_rows, block_rows, 0)
        total = total + lax.ppermute(
            piece, "zl", perm=[(i, (i + shift) % n_zl) for i in range(n_zl)]
        )
    owned = total

    return finish(
        owned[:width_k], owned[width_k + 1], owned[width_k + 2], owned[width_k],
        sample_count,
    )


def solution(mesh):
    n_feat, n_samp = mesh.devices.shape
    n_c, n_zh = 2, 2
    n_x = n_feat // (n_c * n_zh)
    n_zl = 4
    n_y = n_samp // n_zl
    devices = np.asarray(mesh.devices).reshape(n_x, n_zh, n_c, n_y, n_zl)
    fine = Mesh(devices, FEAT_AXES + SAMP_AXES)
    in_specs = (P(FEAT_AXES, SAMP_AXES), P(SAMP_AXES, None), P(None, FEAT_AXES))
    out_specs = P(FEAT_AXES + SAMP_AXES, None)
    return jax.shard_map(
        per_device, mesh=fine, in_specs=in_specs, out_specs=out_specs, check_vma=False
    )
```

```python
import math

import jax
import jax.numpy as jnp
import numpy as np
from jax import lax
from jax.sharding import Mesh
from jax.sharding import PartitionSpec as P

epsilon = 1e-05

FEAT_AXES = ("x", "zh", "c")
SAMP_AXES = ("y", "zl")
EXTRA_ROWS = 8


def combine_rows(first_rows, second_rows, operator_id):
    first_rows = first_rows.astype(jnp.float32)
    second_rows = second_rows.astype(jnp.float32)
    quotient = first_rows / (1.0 + jnp.abs(second_rows))
    built = jnp.where(
        operator_id == 0,
        first_rows + second_rows,
        jnp.where(
            operator_id == 1,
            first_rows - second_rows,
            jnp.where(operator_id == 2, first_rows * second_rows, quotient),
        ),
    )
    return built.astype(jnp.bfloat16)


def ring_gather(block, axis, n):
    assert n == 4
    fwd = [(i, (i + 1) % n) for i in range(n)]
    bwd = [(i, (i - 1) % n) for i in range(n)]
    from_left = lax.ppermute(block, axis, perm=fwd)
    from_right = lax.ppermute(block, axis, perm=bwd)
    half = block.shape[0] // 2
    far_a = lax.ppermute(from_left[:half], axis, perm=fwd)
    far_b = lax.ppermute(from_right[half:], axis, perm=bwd)
    return jnp.concatenate([block, from_right, far_a, far_b, from_left], axis=0)


def finish(product, first_sums, square_sums, col_totals, sample_count):
    means = first_sums / sample_count
    variance = square_sums / sample_count - means * means
    centred = product - means[:, None] * col_totals[None, :]
    return centred * lax.rsqrt(variance + epsilon)[:, None] / math.sqrt(sample_count)


def per_device(tier_one, residuals, pair_list):
    local_rows = tier_one.shape[0]
    local_pairs = pair_list.shape[1]
    width_k = residuals.shape[1]
    n_x = lax.axis_size("x")
    n_zh = lax.axis_size("zh")
    n_y = lax.axis_size("y")
    n_zl = lax.axis_size("zl")
    n_samp = n_y * n_zl
    sample_count = residuals.shape[0] * n_samp

    rows = lax.all_gather(tier_one, "zh", axis=0, tiled=True)
    rows = ring_gather(rows, "x", n_x)
    other = lax.ppermute(rows, "c", perm=[(0, 1), (1, 0)])
    rows = jnp.concatenate([rows, other], axis=0)
    my_c = lax.axis_index("c")
    my_x = lax.axis_index("x")

    def position(g):
        f, r = g // local_rows, g % local_rows
        x, zh, c = f // (2 * n_zh), (f // 2) % n_zh, f % 2
        half = (c != my_c).astype(jnp.int32)
        x_slot = (x - my_x + n_x) % n_x
        return ((half * n_x + x_slot) * n_zh + zh) * local_rows + r

    first_pos = position(pair_list[0])
    second_pos = position(pair_list[1])
    operator_id = pair_list[2]
    col_part = jnp.sum(residuals.astype(jnp.float32), axis=0)

    blocks = local_pairs // width_k
    block_rows = width_k + EXTRA_ROWS
    per_y = local_pairs // n_y
    blocks_per_y = blocks // n_y

    def y_block_terms(dest):
        def pick(v):
            return lax.dynamic_slice_in_dim(v, dest * per_y, per_y, 0)
        first = jnp.take(rows, pick(first_pos), axis=0)
        second = jnp.take(rows, pick(second_pos), axis=0)
        built = combine_rows(first, second, pick(operator_id)[:, None])
        product = jnp.dot(built, residuals, preferred_element_type=jnp.float32)
        widened = built.astype(jnp.float32)
        first_sums = jnp.sum(widened, axis=1)
        square_sums = jnp.sum(widened * widened, axis=1)
        return jnp.concatenate(
            [
                product.reshape(blocks_per_y, width_k, width_k),
                jnp.broadcast_to(col_part[None, None, :], (blocks_per_y, 1, width_k)),
                first_sums.reshape(blocks_per_y, 1, width_k),
                square_sums.reshape(blocks_per_y, 1, width_k),
                jnp.zeros((blocks_per_y, EXTRA_ROWS - 3, width_k), jnp.float32),
            ],
            axis=1,
        ).reshape(blocks_per_y * block_rows, width_k)

    my_y = lax.axis_index("y")
    received = []
    for shift in range(1, n_y):
        dest = (my_y + shift) % n_y
        received.append(lax.ppermute(
            y_block_terms(dest), "y", perm=[(i, (i + shift) % n_y) for i in range(n_y)]
        ))
    owned = y_block_terms(my_y)
    for piece in received:
        owned = owned + piece

    my_zl = lax.axis_index("zl")
    total = lax.dynamic_slice_in_dim(owned, my_zl * block_rows, block_rows, 0)
    for shift in range(1, n_zl):
        dest = (my_zl + shift) % n_zl
        piece = lax.dynamic_slice_in_dim(owned, dest * block_rows, block_rows, 0)
        total = total + lax.ppermute(
            piece, "zl", perm=[(i, (i + shift) % n_zl) for i in range(n_zl)]
        )
    owned = total

    return finish(
        owned[:width_k], owned[width_k + 1], owned[width_k + 2], owned[width_k],
        sample_count,
    )


def solution(mesh):
    n_feat, n_samp = mesh.devices.shape
    n_c, n_zh = 2, 2
    n_x = n_feat // (n_c * n_zh)
    n_zl = 4
    n_y = n_samp // n_zl
    devices = np.asarray(mesh.devices).reshape(n_x, n_zh, n_c, n_y, n_zl)
    fine = Mesh(devices, FEAT_AXES + SAMP_AXES)
    in_specs = (P(FEAT_AXES, SAMP_AXES), P(SAMP_AXES, None), P(None, FEAT_AXES))
    out_specs = P(FEAT_AXES + SAMP_AXES, None)
    return jax.shard_map(
        per_device, mesh=fine, in_specs=in_specs, out_specs=out_specs, check_vma=False
    )
```

```python
import math

import jax
import jax.numpy as jnp
import numpy as np
from jax import lax
from jax.sharding import Mesh
from jax.sharding import PartitionSpec as P

epsilon = 1e-05

FEAT_AXES = ("x", "zh", "c")
SAMP_AXES = ("y", "zl")
EXTRA_ROWS = 8


def combine_rows(first_rows, second_rows, operator_id):
    first_rows = first_rows.astype(jnp.float32)
    second_rows = second_rows.astype(jnp.float32)
    quotient = first_rows / (1.0 + jnp.abs(second_rows))
    built = jnp.where(
        operator_id == 0,
        first_rows + second_rows,
        jnp.where(
            operator_id == 1,
            first_rows - second_rows,
            jnp.where(operator_id == 2, first_rows * second_rows, quotient),
        ),
    )
    return built.astype(jnp.bfloat16)


def ring_gather(block, axis, n):
    assert n == 4
    fwd = [(i, (i + 1) % n) for i in range(n)]
    bwd = [(i, (i - 1) % n) for i in range(n)]
    from_left = lax.ppermute(block, axis, perm=fwd)
    from_right = lax.ppermute(block, axis, perm=bwd)
    half = block.shape[0] // 2
    far_a = lax.ppermute(from_left[:half], axis, perm=fwd)
    far_b = lax.ppermute(from_right[half:], axis, perm=bwd)
    return jnp.concatenate([block, from_right, far_a, far_b, from_left], axis=0)


def finish(product, first_sums, square_sums, col_totals, sample_count):
    means = first_sums / sample_count
    variance = square_sums / sample_count - means * means
    centred = product - means[:, None] * col_totals[None, :]
    return centred * lax.rsqrt(variance + epsilon)[:, None] / math.sqrt(sample_count)


def per_device(tier_one, residuals, pair_list):
    local_rows = tier_one.shape[0]
    local_pairs = pair_list.shape[1]
    width_k = residuals.shape[1]
    n_x = lax.axis_size("x")
    n_zh = lax.axis_size("zh")
    n_y = lax.axis_size("y")
    n_zl = lax.axis_size("zl")
    n_samp = n_y * n_zl
    sample_count = residuals.shape[0] * n_samp

    rows = lax.all_gather(tier_one, "zh", axis=0, tiled=True)
    rows = ring_gather(rows, "x", n_x)
    other = lax.ppermute(rows, "c", perm=[(0, 1), (1, 0)])
    rows = jnp.concatenate([rows, other], axis=0)
    my_c = lax.axis_index("c")
    my_x = lax.axis_index("x")

    def position(g):
        f, r = g // local_rows, g % local_rows
        x, zh, c = f // (2 * n_zh), (f // 2) % n_zh, f % 2
        half = (c != my_c).astype(jnp.int32)
        x_slot = (x - my_x + n_x) % n_x
        return ((half * n_x + x_slot) * n_zh + zh) * local_rows + r

    first = jnp.take(rows, position(pair_list[0]), axis=0)
    second = jnp.take(rows, position(pair_list[1]), axis=0)
    built = combine_rows(first, second, pair_list[2][:, None])

    product = jnp.dot(built, residuals, preferred_element_type=jnp.float32)
    widened = built.astype(jnp.float32)
    first_sums = jnp.sum(widened, axis=1)
    square_sums = jnp.sum(widened * widened, axis=1)
    col_part = jnp.sum(residuals.astype(jnp.float32), axis=0)

    blocks = local_pairs // width_k
    block_rows = width_k + EXTRA_ROWS
    packed = jnp.concatenate(
        [
            product.reshape(blocks, width_k, width_k),
            jnp.broadcast_to(col_part[None, None, :], (blocks, 1, width_k)),
            first_sums.reshape(blocks, 1, width_k),
            square_sums.reshape(blocks, 1, width_k),
            jnp.zeros((blocks, EXTRA_ROWS - 3, width_k), jnp.float32),
        ],
        axis=1,
    ).reshape(blocks * block_rows, width_k)
    arrived = lax.all_to_all(
        packed.reshape(blocks, block_rows, width_k), SAMP_AXES, 0, 0, tiled=False
    )
    owned = jnp.sum(arrived, axis=0)

    return finish(
        owned[:width_k], owned[width_k + 1], owned[width_k + 2], owned[width_k],
        sample_count,
    )


def solution(mesh):
    n_feat, n_samp = mesh.devices.shape
    n_c, n_zh = 2, 2
    n_x = n_feat // (n_c * n_zh)
    n_zl = 4
    n_y = n_samp // n_zl
    devices = np.asarray(mesh.devices).reshape(n_x, n_zh, n_c, n_y, n_zl)
    fine = Mesh(devices, FEAT_AXES + SAMP_AXES)
    in_specs = (P(FEAT_AXES, SAMP_AXES), P(SAMP_AXES, None), P(None, FEAT_AXES))
    out_specs = P(FEAT_AXES + SAMP_AXES, None)
    return jax.shard_map(
        per_device, mesh=fine, in_specs=in_specs, out_specs=out_specs, check_vma=False
    )
```

```python
import math

import jax
import jax.numpy as jnp
import numpy as np
from jax import lax
from jax.sharding import Mesh
from jax.sharding import PartitionSpec as P

epsilon = 1e-05

FEAT_AXES = ("x", "zh", "c")
SAMP_AXES = ("y", "zl")
EXTRA_ROWS = 16


def combine_rows(first_rows, second_rows, operator_id):
    first_rows = first_rows.astype(jnp.float32)
    second_rows = second_rows.astype(jnp.float32)
    quotient = first_rows / (1.0 + jnp.abs(second_rows))
    built = jnp.where(
        operator_id == 0,
        first_rows + second_rows,
        jnp.where(
            operator_id == 1,
            first_rows - second_rows,
            jnp.where(operator_id == 2, first_rows * second_rows, quotient),
        ),
    )
    return built.astype(jnp.bfloat16)


def ring_gather(block, axis, n):
    assert n == 4
    fwd = [(i, (i + 1) % n) for i in range(n)]
    bwd = [(i, (i - 1) % n) for i in range(n)]
    from_left = lax.ppermute(block, axis, perm=fwd)
    from_right = lax.ppermute(block, axis, perm=bwd)
    half = block.shape[0] // 2
    far_a = lax.ppermute(from_left[:half], axis, perm=fwd)
    far_b = lax.ppermute(from_right[half:], axis, perm=bwd)
    return jnp.concatenate([block, from_right, far_a, far_b, from_left], axis=0)


def split3(v):
    hi = lax.reduce_precision(v, exponent_bits=8, mantissa_bits=7)
    rest = v - hi
    mid = lax.reduce_precision(rest, exponent_bits=8, mantissa_bits=7)
    lo = rest - mid
    return jnp.stack([hi, mid, lo], axis=-2).astype(jnp.bfloat16)


def finish(product, first_sums, square_sums, col_totals, sample_count):
    means = first_sums / sample_count
    variance = square_sums / sample_count - means * means
    centred = product - means[:, None] * col_totals[None, :]
    return centred * lax.rsqrt(variance + epsilon)[:, None] / math.sqrt(sample_count)


def per_device(tier_one, residuals, pair_list):
    local_rows = tier_one.shape[0]
    local_pairs = pair_list.shape[1]
    width_k = residuals.shape[1]
    n_x = lax.axis_size("x")
    n_zh = lax.axis_size("zh")
    n_y = lax.axis_size("y")
    n_zl = lax.axis_size("zl")
    n_samp = n_y * n_zl
    sample_count = residuals.shape[0] * n_samp

    rows = lax.all_gather(tier_one, "zh", axis=0, tiled=True)
    rows = ring_gather(rows, "x", n_x)
    other = lax.ppermute(rows, "c", perm=[(0, 1), (1, 0)])
    rows = jnp.concatenate([rows, other], axis=0)
    my_c = lax.axis_index("c")
    my_x = lax.axis_index("x")

    def position(g):
        f, r = g // local_rows, g % local_rows
        x, zh, c = f // (2 * n_zh), (f // 2) % n_zh, f % 2
        half = (c != my_c).astype(jnp.int32)
        x_slot = (x - my_x + n_x) % n_x
        return ((half * n_x + x_slot) * n_zh + zh) * local_rows + r

    first = jnp.take(rows, position(pair_list[0]), axis=0)
    second = jnp.take(rows, position(pair_list[1]), axis=0)
    built = combine_rows(first, second, pair_list[2][:, None])

    product = jnp.dot(built, residuals, preferred_element_type=jnp.float32)
    widened = built.astype(jnp.float32)
    first_sums = jnp.sum(widened, axis=1)
    square_sums = jnp.sum(widened * widened, axis=1)
    col_part = jnp.sum(residuals.astype(jnp.float32), axis=0)
    local_samples = residuals.shape[0]

    local_means = first_sums / local_samples
    centred = product - local_means[:, None] * col_part[None, :]

    blocks = local_pairs // width_k
    block_rows = width_k + EXTRA_ROWS
    extras = jnp.concatenate(
        [
            split3(jnp.broadcast_to(col_part[None, :], (blocks, width_k))),
            split3(first_sums.reshape(blocks, width_k)),
            split3(square_sums.reshape(blocks, width_k)),
            jnp.zeros((blocks, EXTRA_ROWS - 9, width_k), jnp.bfloat16),
        ],
        axis=1,
    )
    packed = jnp.concatenate(
        [centred.astype(jnp.bfloat16).reshape(blocks, width_k, width_k), extras], axis=1
    )
    arrived = lax.all_to_all(packed, SAMP_AXES, 0, 0, tiled=False)
    centred_sum = jnp.sum(arrived[:, :width_k].astype(jnp.float32), axis=0)
    pieces = arrived[:, width_k:].astype(jnp.float32)

    def joined(i):
        return (pieces[:, i] + pieces[:, i + 1]) + pieces[:, i + 2]

    col_parts, first_parts, square_parts = joined(0), joined(3), joined(6)
    mean_share = jnp.einsum(
        "dp,dk->pk", first_parts / local_samples, col_parts,
        precision=lax.Precision.HIGHEST,
    )
    return finish(
        centred_sum + mean_share,
        jnp.sum(first_parts, axis=0),
        jnp.sum(square_parts, axis=0),
        jnp.sum(col_parts, axis=0),
        sample_count,
    )


def solution(mesh):
    n_feat, n_samp = mesh.devices.shape
    n_c, n_zh = 2, 2
    n_x = n_feat // (n_c * n_zh)
    n_zl = 4
    n_y = n_samp // n_zl
    devices = np.asarray(mesh.devices).reshape(n_x, n_zh, n_c, n_y, n_zl)
    fine = Mesh(devices, FEAT_AXES + SAMP_AXES)
    in_specs = (P(FEAT_AXES, SAMP_AXES), P(SAMP_AXES, None), P(None, FEAT_AXES))
    out_specs = P(FEAT_AXES + SAMP_AXES, None)
    return jax.shard_map(
        per_device, mesh=fine, in_specs=in_specs, out_specs=out_specs, check_vma=False
    )
```

```python
import math

import jax
import jax.numpy as jnp
import numpy as np
from jax import lax
from jax.sharding import Mesh
from jax.sharding import PartitionSpec as P

epsilon = 1e-05

FEAT_AXES = ("x", "zh", "c")
SAMP_AXES = ("y", "zl")
EXTRA_ROWS = 16


def combine_rows(first_rows, second_rows, operator_id):
    first_rows = first_rows.astype(jnp.float32)
    second_rows = second_rows.astype(jnp.float32)
    quotient = first_rows / (1.0 + jnp.abs(second_rows))
    built = jnp.where(
        operator_id == 0,
        first_rows + second_rows,
        jnp.where(
            operator_id == 1,
            first_rows - second_rows,
            jnp.where(operator_id == 2, first_rows * second_rows, quotient),
        ),
    )
    return built.astype(jnp.bfloat16)


def ring_gather(block, axis, n):
    assert n == 4
    fwd = [(i, (i + 1) % n) for i in range(n)]
    bwd = [(i, (i - 1) % n) for i in range(n)]
    from_left = lax.ppermute(block, axis, perm=fwd)
    from_right = lax.ppermute(block, axis, perm=bwd)
    half = block.shape[0] // 2
    far_a = lax.ppermute(from_left[:half], axis, perm=fwd)
    far_b = lax.ppermute(from_right[half:], axis, perm=bwd)
    return jnp.concatenate([block, from_right, far_a, far_b, from_left], axis=0)


def split3(v):
    hi = lax.reduce_precision(v, exponent_bits=8, mantissa_bits=7)
    rest = v - hi
    mid = lax.reduce_precision(rest, exponent_bits=8, mantissa_bits=7)
    lo = rest - mid
    return jnp.stack([hi, mid, lo], axis=-2).astype(jnp.bfloat16)


def finish(product, first_sums, square_sums, col_totals, sample_count):
    means = first_sums / sample_count
    variance = square_sums / sample_count - means * means
    centred = product - means[:, None] * col_totals[None, :]
    return centred * lax.rsqrt(variance + epsilon)[:, None] / math.sqrt(sample_count)


def per_device(tier_one, residuals, pair_list):
    local_rows = tier_one.shape[0]
    local_pairs = pair_list.shape[1]
    width_k = residuals.shape[1]
    n_x = lax.axis_size("x")
    n_zh = lax.axis_size("zh")
    n_y = lax.axis_size("y")
    n_zl = lax.axis_size("zl")
    n_samp = n_y * n_zl
    sample_count = residuals.shape[0] * n_samp

    my_zh = lax.axis_index("zh")
    my_c = lax.axis_index("c")
    my_x = lax.axis_index("x")

    own_ring = ring_gather(tier_one, "x", n_x)
    pair_rows = lax.all_gather(tier_one, "zh", axis=0, tiled=True)
    partner = lax.dynamic_slice_in_dim(pair_rows, (1 - my_zh) * local_rows, local_rows, 0)
    partner_ring = ring_gather(partner, "x", n_x)
    swap = [(0, 1), (1, 0)]
    rows = jnp.concatenate(
        [
            own_ring,
            partner_ring,
            lax.ppermute(own_ring, "c", perm=swap),
            lax.ppermute(partner_ring, "c", perm=swap),
        ],
        axis=0,
    )

    def position(g):
        f, r = g // local_rows, g % local_rows
        x, zh, c = f // (2 * n_zh), (f // 2) % n_zh, f % 2
        c_half = (c != my_c).astype(jnp.int32)
        zh_half = (zh != my_zh).astype(jnp.int32)
        x_slot = (x - my_x + n_x) % n_x
        return ((c_half * n_zh + zh_half) * n_x + x_slot) * local_rows + r

    first = jnp.take(rows, position(pair_list[0]), axis=0)
    second = jnp.take(rows, position(pair_list[1]), axis=0)
    built = combine_rows(first, second, pair_list[2][:, None])

    product = jnp.dot(built, residuals, preferred_element_type=jnp.float32)
    widened = built.astype(jnp.float32)
    first_sums = jnp.sum(widened, axis=1)
    square_sums = jnp.sum(widened * widened, axis=1)
    col_part = jnp.sum(residuals.astype(jnp.float32), axis=0)
    local_samples = residuals.shape[0]

    local_means = first_sums / local_samples
    centred = product - local_means[:, None] * col_part[None, :]

    blocks = local_pairs // width_k
    block_rows = width_k + EXTRA_ROWS
    extras = jnp.concatenate(
        [
            split3(jnp.broadcast_to(col_part[None, :], (blocks, width_k))),
            split3(first_sums.reshape(blocks, width_k)),
            split3(square_sums.reshape(blocks, width_k)),
            jnp.zeros((blocks, EXTRA_ROWS - 9, width_k), jnp.bfloat16),
        ],
        axis=1,
    )
    packed = jnp.concatenate(
        [centred.astype(jnp.bfloat16).reshape(blocks, width_k, width_k), extras], axis=1
    )
    arrived = lax.all_to_all(packed, SAMP_AXES, 0, 0, tiled=False)
    centred_sum = jnp.sum(arrived[:, :width_k].astype(jnp.float32), axis=0)
    pieces = arrived[:, width_k:].astype(jnp.float32)

    def joined(i):
        return (pieces[:, i] + pieces[:, i + 1]) + pieces[:, i + 2]

    col_parts, first_parts, square_parts = joined(0), joined(3), joined(6)
    mean_share = jnp.einsum(
        "dp,dk->pk", first_parts / local_samples, col_parts,
        precision=lax.Precision.HIGHEST,
    )
    return finish(
        centred_sum + mean_share,
        jnp.sum(first_parts, axis=0),
        jnp.sum(square_parts, axis=0),
        jnp.sum(col_parts, axis=0),
        sample_count,
    )


def solution(mesh):
    n_feat, n_samp = mesh.devices.shape
    n_c, n_zh = 2, 2
    n_x = n_feat // (n_c * n_zh)
    n_zl = 4
    n_y = n_samp // n_zl
    devices = np.asarray(mesh.devices).reshape(n_x, n_zh, n_c, n_y, n_zl)
    fine = Mesh(devices, FEAT_AXES + SAMP_AXES)
    in_specs = (P(FEAT_AXES, SAMP_AXES), P(SAMP_AXES, None), P(None, FEAT_AXES))
    out_specs = P(FEAT_AXES + SAMP_AXES, None)
    return jax.shard_map(
        per_device, mesh=fine, in_specs=in_specs, out_specs=out_specs, check_vma=False
    )
```

```python
import math

import jax
import jax.numpy as jnp
import numpy as np
from jax import lax
from jax.sharding import Mesh
from jax.sharding import PartitionSpec as P

epsilon = 1e-05

FEAT_AXES = ("x", "zh", "c")
SAMP_AXES = ("y", "zl")
EXTRA_ROWS = 16


def combine_rows(first_rows, second_rows, operator_id):
    first_rows = first_rows.astype(jnp.float32)
    second_rows = second_rows.astype(jnp.float32)
    quotient = first_rows / (1.0 + jnp.abs(second_rows))
    built = jnp.where(
        operator_id == 0,
        first_rows + second_rows,
        jnp.where(
            operator_id == 1,
            first_rows - second_rows,
            jnp.where(operator_id == 2, first_rows * second_rows, quotient),
        ),
    )
    return built.astype(jnp.bfloat16)


def ring_gather(block, axis, n):
    assert n == 4
    fwd = [(i, (i + 1) % n) for i in range(n)]
    bwd = [(i, (i - 1) % n) for i in range(n)]
    from_left = lax.ppermute(block, axis, perm=fwd)
    from_right = lax.ppermute(block, axis, perm=bwd)
    half = block.shape[0] // 2
    far_a = lax.ppermute(from_left[:half], axis, perm=fwd)
    far_b = lax.ppermute(from_right[half:], axis, perm=bwd)
    return jnp.concatenate([block, from_right, far_a, far_b, from_left], axis=0)


def split3(v):
    hi = lax.reduce_precision(v, exponent_bits=8, mantissa_bits=7)
    rest = v - hi
    mid = lax.reduce_precision(rest, exponent_bits=8, mantissa_bits=7)
    lo = rest - mid
    return jnp.stack([hi, mid, lo], axis=-2).astype(jnp.bfloat16)


def finish(product, first_sums, square_sums, col_totals, sample_count):
    means = first_sums / sample_count
    variance = square_sums / sample_count - means * means
    centred = product - means[:, None] * col_totals[None, :]
    return centred * lax.rsqrt(variance + epsilon)[:, None] / math.sqrt(sample_count)


def per_device(tier_one, residuals, pair_list):
    local_rows = tier_one.shape[0]
    local_pairs = pair_list.shape[1]
    width_k = residuals.shape[1]
    n_x = lax.axis_size("x")
    n_zh = lax.axis_size("zh")
    n_y = lax.axis_size("y")
    n_zl = lax.axis_size("zl")
    n_samp = n_y * n_zl
    sample_count = residuals.shape[0] * n_samp

    rows = lax.all_gather(tier_one, "zh", axis=0, tiled=True)
    rows = lax.all_to_all(
        jnp.broadcast_to(rows[None], (n_x,) + rows.shape), "x", 0, 0, tiled=False
    ).reshape(n_x * rows.shape[0], rows.shape[1])
    other = lax.ppermute(rows, "c", perm=[(0, 1), (1, 0)])
    rows = jnp.concatenate([rows, other], axis=0)
    my_c = lax.axis_index("c")
    my_x = lax.axis_index("x")

    def position(g):
        f, r = g // local_rows, g % local_rows
        x, zh, c = f // (2 * n_zh), (f // 2) % n_zh, f % 2
        half = (c != my_c).astype(jnp.int32)
        return ((half * n_x + x) * n_zh + zh) * local_rows + r

    first = jnp.take(rows, position(pair_list[0]), axis=0)
    second = jnp.take(rows, position(pair_list[1]), axis=0)
    built = combine_rows(first, second, pair_list[2][:, None])

    product = jnp.dot(built, residuals, preferred_element_type=jnp.float32)
    widened = built.astype(jnp.float32)
    first_sums = jnp.sum(widened, axis=1)
    square_sums = jnp.sum(widened * widened, axis=1)
    col_part = jnp.sum(residuals.astype(jnp.float32), axis=0)
    local_samples = residuals.shape[0]

    local_means = first_sums / local_samples
    centred = product - local_means[:, None] * col_part[None, :]

    blocks = local_pairs // width_k
    block_rows = width_k + EXTRA_ROWS
    extras = jnp.concatenate(
        [
            split3(jnp.broadcast_to(col_part[None, :], (blocks, width_k))),
            split3(first_sums.reshape(blocks, width_k)),
            split3(square_sums.reshape(blocks, width_k)),
            jnp.zeros((blocks, EXTRA_ROWS - 9, width_k), jnp.bfloat16),
        ],
        axis=1,
    )
    packed = jnp.concatenate(
        [centred.astype(jnp.bfloat16).reshape(blocks, width_k, width_k), extras], axis=1
    )
    arrived = lax.all_to_all(packed, SAMP_AXES, 0, 0, tiled=False)
    centred_sum = jnp.sum(arrived[:, :width_k].astype(jnp.float32), axis=0)
    pieces = arrived[:, width_k:].astype(jnp.float32)

    def joined(i):
        return (pieces[:, i] + pieces[:, i + 1]) + pieces[:, i + 2]

    col_parts, first_parts, square_parts = joined(0), joined(3), joined(6)
    mean_share = jnp.einsum(
        "dp,dk->pk", first_parts / local_samples, col_parts,
        precision=lax.Precision.HIGHEST,
    )
    return finish(
        centred_sum + mean_share,
        jnp.sum(first_parts, axis=0),
        jnp.sum(square_parts, axis=0),
        jnp.sum(col_parts, axis=0),
        sample_count,
    )


def solution(mesh):
    n_feat, n_samp = mesh.devices.shape
    n_c, n_zh = 2, 2
    n_x = n_feat // (n_c * n_zh)
    n_zl = 4
    n_y = n_samp // n_zl
    devices = np.asarray(mesh.devices).reshape(n_x, n_zh, n_c, n_y, n_zl)
    fine = Mesh(devices, FEAT_AXES + SAMP_AXES)
    in_specs = (P(FEAT_AXES, SAMP_AXES), P(SAMP_AXES, None), P(None, FEAT_AXES))
    out_specs = P(FEAT_AXES + SAMP_AXES, None)
    return jax.shard_map(
        per_device, mesh=fine, in_specs=in_specs, out_specs=out_specs, check_vma=False
    )
```

```python
import math

import jax
import jax.numpy as jnp
from jax.experimental import pallas as pl
from jax.experimental.pallas import tpu as pltpu
import numpy as np
from jax import lax
from jax.sharding import Mesh
from jax.sharding import PartitionSpec as P

epsilon = 1e-05

FEAT_AXES = ("x", "zh", "c")
SAMP_AXES = ("y", "zl")
EXTRA_ROWS = 16
GATHER_TILE = 512


def combine_rows(first_rows, second_rows, operator_id):
    first_rows = first_rows.astype(jnp.float32)
    second_rows = second_rows.astype(jnp.float32)
    quotient = first_rows / (1.0 + jnp.abs(second_rows))
    built = jnp.where(
        operator_id == 0,
        first_rows + second_rows,
        jnp.where(
            operator_id == 1,
            first_rows - second_rows,
            jnp.where(operator_id == 2, first_rows * second_rows, quotient),
        ),
    )
    return built.astype(jnp.bfloat16)


def gather_kernel(first_ref, second_ref, table_ref, op_ref, out_ref, first_buf, second_buf):
    tile = first_buf.shape[0]
    base = pl.program_id(0) * tile
    def body(j, carry):
        a = first_ref[base + j]
        b = second_ref[base + j]
        first_buf[pl.ds(j, 1), :] = table_ref[pl.ds(a, 1), :]
        second_buf[pl.ds(j, 1), :] = table_ref[pl.ds(b, 1), :]
        return carry
    lax.fori_loop(0, tile, body, 0, unroll=8)
    out_ref[...] = combine_rows(first_buf[...], second_buf[...], op_ref[...])

def build_descriptors(table, first_pos, second_pos, operator_id):
    n_rows, width = table.shape
    pairs = first_pos.shape[0]
    tile = min(GATHER_TILE, pairs)
    grid_spec = pltpu.PrefetchScalarGridSpec(
        num_scalar_prefetch=2,
        grid=(pairs // tile,),
        in_specs=[
            pl.BlockSpec((n_rows, width), lambda i, p1, p2: (0, 0)),
            pl.BlockSpec((tile, 1), lambda i, p1, p2: (i, 0)),
        ],
        out_specs=pl.BlockSpec((tile, width), lambda i, p1, p2: (i, 0)),
        scratch_shapes=[pltpu.VMEM((tile, width), jnp.float32)] * 2,
    )
    return pl.pallas_call(
        gather_kernel,
        grid_spec=grid_spec,
        out_shape=jax.ShapeDtypeStruct((pairs, width), jnp.bfloat16),
        compiler_params=pltpu.CompilerParams(vmem_limit_bytes=60 * 1024 * 1024),
        cost_estimate=pl.CostEstimate(
            flops=10 * pairs * width, transcendentals=0,
            bytes_accessed=n_rows * width * 4 + pairs * width * 2),
    )(first_pos, second_pos, table.astype(jnp.float32), operator_id[:, None])


def ring_gather(block, axis, n):
    assert n == 4
    fwd = [(i, (i + 1) % n) for i in range(n)]
    bwd = [(i, (i - 1) % n) for i in range(n)]
    from_left = lax.ppermute(block, axis, perm=fwd)
    from_right = lax.ppermute(block, axis, perm=bwd)
    half = block.shape[0] // 2
    far_a = lax.ppermute(from_left[:half], axis, perm=fwd)
    far_b = lax.ppermute(from_right[half:], axis, perm=bwd)
    return jnp.concatenate([block, from_right, far_a, far_b, from_left], axis=0)


def split3(v):
    hi = lax.reduce_precision(v, exponent_bits=8, mantissa_bits=7)
    rest = v - hi
    mid = lax.reduce_precision(rest, exponent_bits=8, mantissa_bits=7)
    lo = rest - mid
    return jnp.stack([hi, mid, lo], axis=-2).astype(jnp.bfloat16)


def finish(product, first_sums, square_sums, col_totals, sample_count):
    means = first_sums / sample_count
    variance = square_sums / sample_count - means * means
    centred = product - means[:, None] * col_totals[None, :]
    return centred * lax.rsqrt(variance + epsilon)[:, None] / math.sqrt(sample_count)


def per_device(tier_one, residuals, pair_list):
    local_rows = tier_one.shape[0]
    local_pairs = pair_list.shape[1]
    width_k = residuals.shape[1]
    n_x = lax.axis_size("x")
    n_zh = lax.axis_size("zh")
    n_y = lax.axis_size("y")
    n_zl = lax.axis_size("zl")
    n_samp = n_y * n_zl
    sample_count = residuals.shape[0] * n_samp

    rows = lax.all_gather(tier_one, "zh", axis=0, tiled=True)
    rows = ring_gather(rows, "x", n_x)
    other = lax.ppermute(rows, "c", perm=[(0, 1), (1, 0)])
    rows = jnp.concatenate([rows, other], axis=0)
    my_c = lax.axis_index("c")
    my_x = lax.axis_index("x")

    def position(g):
        f, r = g // local_rows, g % local_rows
        x, zh, c = f // (2 * n_zh), (f // 2) % n_zh, f % 2
        half = (c != my_c).astype(jnp.int32)
        x_slot = (x - my_x + n_x) % n_x
        return ((half * n_x + x_slot) * n_zh + zh) * local_rows + r

    built = build_descriptors(
        rows, position(pair_list[0]), position(pair_list[1]), pair_list[2]
    )

    product = jnp.dot(built, residuals, preferred_element_type=jnp.float32)
    widened = built.astype(jnp.float32)
    first_sums = jnp.sum(widened, axis=1)
    square_sums = jnp.sum(widened * widened, axis=1)
    col_part = jnp.sum(residuals.astype(jnp.float32), axis=0)
    local_samples = residuals.shape[0]

    local_means = first_sums / local_samples
    centred = product - local_means[:, None] * col_part[None, :]

    blocks = local_pairs // width_k
    block_rows = width_k + EXTRA_ROWS
    extras = jnp.concatenate(
        [
            split3(jnp.broadcast_to(col_part[None, :], (blocks, width_k))),
            split3(first_sums.reshape(blocks, width_k)),
            split3(square_sums.reshape(blocks, width_k)),
            jnp.zeros((blocks, EXTRA_ROWS - 9, width_k), jnp.bfloat16),
        ],
        axis=1,
    )
    packed = jnp.concatenate(
        [centred.astype(jnp.bfloat16).reshape(blocks, width_k, width_k), extras], axis=1
    )
    arrived = lax.all_to_all(packed, SAMP_AXES, 0, 0, tiled=False)
    centred_sum = jnp.sum(arrived[:, :width_k].astype(jnp.float32), axis=0)
    pieces = arrived[:, width_k:].astype(jnp.float32)

    def joined(i):
        return (pieces[:, i] + pieces[:, i + 1]) + pieces[:, i + 2]

    col_parts, first_parts, square_parts = joined(0), joined(3), joined(6)
    mean_share = jnp.einsum(
        "dp,dk->pk", first_parts / local_samples, col_parts,
        precision=lax.Precision.HIGHEST,
    )
    return finish(
        centred_sum + mean_share,
        jnp.sum(first_parts, axis=0),
        jnp.sum(square_parts, axis=0),
        jnp.sum(col_parts, axis=0),
        sample_count,
    )


def solution(mesh):
    n_feat, n_samp = mesh.devices.shape
    n_c, n_zh = 2, 2
    n_x = n_feat // (n_c * n_zh)
    n_zl = 4
    n_y = n_samp // n_zl
    devices = np.asarray(mesh.devices).reshape(n_x, n_zh, n_c, n_y, n_zl)
    fine = Mesh(devices, FEAT_AXES + SAMP_AXES)
    in_specs = (P(FEAT_AXES, SAMP_AXES), P(SAMP_AXES, None), P(None, FEAT_AXES))
    out_specs = P(FEAT_AXES + SAMP_AXES, None)
    return jax.shard_map(
        per_device, mesh=fine, in_specs=in_specs, out_specs=out_specs, check_vma=False
    )
```

```python
import math

import jax
import jax.numpy as jnp
from jax.experimental import pallas as pl
from jax.experimental.pallas import tpu as pltpu
import numpy as np
from jax import lax
from jax.sharding import Mesh
from jax.sharding import PartitionSpec as P

epsilon = 1e-05

FEAT_AXES = ("x", "zh", "c")
SAMP_AXES = ("y", "zl")
EXTRA_ROWS = 16
GATHER_TILE = 512


def combine_rows(first_rows, second_rows, operator_id):
    first_rows = first_rows.astype(jnp.float32)
    second_rows = second_rows.astype(jnp.float32)
    quotient = first_rows / (1.0 + jnp.abs(second_rows))
    built = jnp.where(
        operator_id == 0,
        first_rows + second_rows,
        jnp.where(
            operator_id == 1,
            first_rows - second_rows,
            jnp.where(operator_id == 2, first_rows * second_rows, quotient),
        ),
    )
    return built.astype(jnp.bfloat16)


def gather_kernel(first_ref, second_ref, table_ref, op_ref, out_ref, table, first_buf, second_buf):
    tile = first_buf.shape[0]
    step = 256

    @pl.when(pl.program_id(0) == 0)
    def _():
        def widen(i, carry):
            rows = pl.ds(pl.multiple_of(i * step, step), step)
            table[rows, :] = table_ref[rows, :].astype(jnp.float32)
            return carry
        lax.fori_loop(0, table.shape[0] // step, widen, 0)

    base = pl.program_id(0) * tile

    def body(j, carry):
        a = first_ref[base + j]
        b = second_ref[base + j]
        first_buf[pl.ds(j, 1), :] = table[pl.ds(a, 1), :]
        second_buf[pl.ds(j, 1), :] = table[pl.ds(b, 1), :]
        return carry

    lax.fori_loop(0, tile, body, 0, unroll=8)
    out_ref[...] = combine_rows(first_buf[...], second_buf[...], op_ref[...])


def build_descriptors(table, first_pos, second_pos, operator_id):
    n_rows, width = table.shape
    pairs = first_pos.shape[0]
    tile = min(GATHER_TILE, pairs)
    grid_spec = pltpu.PrefetchScalarGridSpec(
        num_scalar_prefetch=2,
        grid=(pairs // tile,),
        in_specs=[
            pl.BlockSpec((n_rows, width), lambda i, p1, p2: (0, 0)),
            pl.BlockSpec((tile, 1), lambda i, p1, p2: (i, 0)),
        ],
        out_specs=pl.BlockSpec((tile, width), lambda i, p1, p2: (i, 0)),
        scratch_shapes=[pltpu.VMEM((n_rows, width), jnp.float32)]
        + [pltpu.VMEM((tile, width), jnp.float32)] * 2,
    )
    return pl.pallas_call(
        gather_kernel,
        grid_spec=grid_spec,
        out_shape=jax.ShapeDtypeStruct((pairs, width), jnp.bfloat16),
        compiler_params=pltpu.CompilerParams(
            dimension_semantics=("arbitrary",), vmem_limit_bytes=60 * 1024 * 1024
        ),
        cost_estimate=pl.CostEstimate(
            flops=10 * pairs * width, transcendentals=0,
            bytes_accessed=n_rows * width * 2 + pairs * width * 2),
    )(first_pos, second_pos, table, operator_id[:, None])


def ring_gather(block, axis, n):
    assert n == 4
    fwd = [(i, (i + 1) % n) for i in range(n)]
    bwd = [(i, (i - 1) % n) for i in range(n)]
    from_left = lax.ppermute(block, axis, perm=fwd)
    from_right = lax.ppermute(block, axis, perm=bwd)
    half = block.shape[0] // 2
    far_a = lax.ppermute(from_left[:half], axis, perm=fwd)
    far_b = lax.ppermute(from_right[half:], axis, perm=bwd)
    return jnp.concatenate([block, from_right, far_a, far_b, from_left], axis=0)


def split3(v):
    hi = lax.reduce_precision(v, exponent_bits=8, mantissa_bits=7)
    rest = v - hi
    mid = lax.reduce_precision(rest, exponent_bits=8, mantissa_bits=7)
    lo = rest - mid
    return jnp.stack([hi, mid, lo], axis=-2).astype(jnp.bfloat16)


def finish(product, first_sums, square_sums, col_totals, sample_count):
    means = first_sums / sample_count
    variance = square_sums / sample_count - means * means
    centred = product - means[:, None] * col_totals[None, :]
    return centred * lax.rsqrt(variance + epsilon)[:, None] / math.sqrt(sample_count)


def per_device(tier_one, residuals, pair_list):
    local_rows = tier_one.shape[0]
    local_pairs = pair_list.shape[1]
    width_k = residuals.shape[1]
    n_x = lax.axis_size("x")
    n_zh = lax.axis_size("zh")
    n_y = lax.axis_size("y")
    n_zl = lax.axis_size("zl")
    n_samp = n_y * n_zl
    sample_count = residuals.shape[0] * n_samp

    rows = lax.all_gather(tier_one, "zh", axis=0, tiled=True)
    rows = ring_gather(rows, "x", n_x)
    other = lax.ppermute(rows, "c", perm=[(0, 1), (1, 0)])
    rows = jnp.concatenate([rows, other], axis=0)
    my_c = lax.axis_index("c")
    my_x = lax.axis_index("x")

    def position(g):
        f, r = g // local_rows, g % local_rows
        x, zh, c = f // (2 * n_zh), (f // 2) % n_zh, f % 2
        half = (c != my_c).astype(jnp.int32)
        x_slot = (x - my_x + n_x) % n_x
        return ((half * n_x + x_slot) * n_zh + zh) * local_rows + r

    built = build_descriptors(
        rows, position(pair_list[0]), position(pair_list[1]), pair_list[2]
    )

    product = jnp.dot(built, residuals, preferred_element_type=jnp.float32)
    widened = built.astype(jnp.float32)
    first_sums = jnp.sum(widened, axis=1)
    square_sums = jnp.sum(widened * widened, axis=1)
    col_part = jnp.sum(residuals.astype(jnp.float32), axis=0)
    local_samples = residuals.shape[0]

    local_means = first_sums / local_samples
    centred = product - local_means[:, None] * col_part[None, :]

    blocks = local_pairs // width_k
    block_rows = width_k + EXTRA_ROWS
    extras = jnp.concatenate(
        [
            split3(jnp.broadcast_to(col_part[None, :], (blocks, width_k))),
            split3(first_sums.reshape(blocks, width_k)),
            split3(square_sums.reshape(blocks, width_k)),
            jnp.zeros((blocks, EXTRA_ROWS - 9, width_k), jnp.bfloat16),
        ],
        axis=1,
    )
    packed = jnp.concatenate(
        [centred.astype(jnp.bfloat16).reshape(blocks, width_k, width_k), extras], axis=1
    )
    arrived = lax.all_to_all(packed, SAMP_AXES, 0, 0, tiled=False)
    centred_sum = jnp.sum(arrived[:, :width_k].astype(jnp.float32), axis=0)
    pieces = arrived[:, width_k:].astype(jnp.float32)

    def joined(i):
        return (pieces[:, i] + pieces[:, i + 1]) + pieces[:, i + 2]

    col_parts, first_parts, square_parts = joined(0), joined(3), joined(6)
    mean_share = jnp.einsum(
        "dp,dk->pk", first_parts / local_samples, col_parts,
        precision=lax.Precision.HIGHEST,
    )
    return finish(
        centred_sum + mean_share,
        jnp.sum(first_parts, axis=0),
        jnp.sum(square_parts, axis=0),
        jnp.sum(col_parts, axis=0),
        sample_count,
    )


def solution(mesh):
    n_feat, n_samp = mesh.devices.shape
    n_c, n_zh = 2, 2
    n_x = n_feat // (n_c * n_zh)
    n_zl = 4
    n_y = n_samp // n_zl
    devices = np.asarray(mesh.devices).reshape(n_x, n_zh, n_c, n_y, n_zl)
    fine = Mesh(devices, FEAT_AXES + SAMP_AXES)
    in_specs = (P(FEAT_AXES, SAMP_AXES), P(SAMP_AXES, None), P(None, FEAT_AXES))
    out_specs = P(FEAT_AXES + SAMP_AXES, None)
    return jax.shard_map(
        per_device, mesh=fine, in_specs=in_specs, out_specs=out_specs, check_vma=False
    )
```

```python
import math

import jax
import jax.numpy as jnp
from jax.experimental import pallas as pl
from jax.experimental.pallas import tpu as pltpu
import numpy as np
from jax import lax
from jax.sharding import Mesh
from jax.sharding import PartitionSpec as P

epsilon = 1e-05

FEAT_AXES = ("x", "zh", "c")
SAMP_AXES = ("y", "zl")
EXTRA_ROWS = 16
GATHER_TILE = 512


def combine_rows(first_rows, second_rows, operator_id):
    first_rows = first_rows.astype(jnp.float32)
    second_rows = second_rows.astype(jnp.float32)
    quotient = first_rows / (1.0 + jnp.abs(second_rows))
    built = jnp.where(
        operator_id == 0,
        first_rows + second_rows,
        jnp.where(
            operator_id == 1,
            first_rows - second_rows,
            jnp.where(operator_id == 2, first_rows * second_rows, quotient),
        ),
    )
    return built.astype(jnp.bfloat16)


def gather_kernel(first_ref, second_ref, table_ref, op_ref, out_ref, table, first_buf, second_buf):
    tile = first_buf.shape[0]
    step = 256

    @pl.when(pl.program_id(0) == 0)
    def _():
        def widen(i, carry):
            rows = pl.ds(pl.multiple_of(i * step, step), step)
            table[rows, :] = table_ref[rows, :].astype(jnp.float32)
            return carry
        lax.fori_loop(0, table.shape[0] // step, widen, 0)

    base = pl.program_id(0) * tile

    def body(g, carry):
        j0 = pl.multiple_of(g * 8, 8)
        firsts, seconds = [], []
        for t in range(8):
            firsts.append(table[pl.ds(first_ref[base + j0 + t], 1), :])
            seconds.append(table[pl.ds(second_ref[base + j0 + t], 1), :])
        first_buf[pl.ds(j0, 8), :] = jnp.concatenate(firsts, axis=0)
        second_buf[pl.ds(j0, 8), :] = jnp.concatenate(seconds, axis=0)
        return carry

    lax.fori_loop(0, tile // 8, body, 0)
    out_ref[...] = combine_rows(first_buf[...], second_buf[...], op_ref[...])


def build_descriptors(table, first_pos, second_pos, operator_id):
    n_rows, width = table.shape
    pairs = first_pos.shape[0]
    tile = min(GATHER_TILE, pairs)
    grid_spec = pltpu.PrefetchScalarGridSpec(
        num_scalar_prefetch=2,
        grid=(pairs // tile,),
        in_specs=[
            pl.BlockSpec((n_rows, width), lambda i, p1, p2: (0, 0)),
            pl.BlockSpec((tile, 1), lambda i, p1, p2: (i, 0)),
        ],
        out_specs=pl.BlockSpec((tile, width), lambda i, p1, p2: (i, 0)),
        scratch_shapes=[pltpu.VMEM((n_rows, width), jnp.float32)]
        + [pltpu.VMEM((tile, width), jnp.float32)] * 2,
    )
    return pl.pallas_call(
        gather_kernel,
        grid_spec=grid_spec,
        out_shape=jax.ShapeDtypeStruct((pairs, width), jnp.bfloat16),
        compiler_params=pltpu.CompilerParams(
            dimension_semantics=("arbitrary",), vmem_limit_bytes=60 * 1024 * 1024
        ),
        cost_estimate=pl.CostEstimate(
            flops=10 * pairs * width, transcendentals=0,
            bytes_accessed=n_rows * width * 2 + pairs * width * 2),
    )(first_pos, second_pos, table, operator_id[:, None])


def ring_gather(block, axis, n):
    assert n == 4
    fwd = [(i, (i + 1) % n) for i in range(n)]
    bwd = [(i, (i - 1) % n) for i in range(n)]
    from_left = lax.ppermute(block, axis, perm=fwd)
    from_right = lax.ppermute(block, axis, perm=bwd)
    half = block.shape[0] // 2
    far_a = lax.ppermute(from_left[:half], axis, perm=fwd)
    far_b = lax.ppermute(from_right[half:], axis, perm=bwd)
    return jnp.concatenate([block, from_right, far_a, far_b, from_left], axis=0)


def split3(v):
    hi = lax.reduce_precision(v, exponent_bits=8, mantissa_bits=7)
    rest = v - hi
    mid = lax.reduce_precision(rest, exponent_bits=8, mantissa_bits=7)
    lo = rest - mid
    return jnp.stack([hi, mid, lo], axis=-2).astype(jnp.bfloat16)


def finish(product, first_sums, square_sums, col_totals, sample_count):
    means = first_sums / sample_count
    variance = square_sums / sample_count - means * means
    centred = product - means[:, None] * col_totals[None, :]
    return centred * lax.rsqrt(variance + epsilon)[:, None] / math.sqrt(sample_count)


def per_device(tier_one, residuals, pair_list):
    local_rows = tier_one.shape[0]
    local_pairs = pair_list.shape[1]
    width_k = residuals.shape[1]
    n_x = lax.axis_size("x")
    n_zh = lax.axis_size("zh")
    n_y = lax.axis_size("y")
    n_zl = lax.axis_size("zl")
    n_samp = n_y * n_zl
    sample_count = residuals.shape[0] * n_samp

    rows = lax.all_gather(tier_one, "zh", axis=0, tiled=True)
    rows = ring_gather(rows, "x", n_x)
    other = lax.ppermute(rows, "c", perm=[(0, 1), (1, 0)])
    rows = jnp.concatenate([rows, other], axis=0)
    my_c = lax.axis_index("c")
    my_x = lax.axis_index("x")

    def position(g):
        f, r = g // local_rows, g % local_rows
        x, zh, c = f // (2 * n_zh), (f // 2) % n_zh, f % 2
        half = (c != my_c).astype(jnp.int32)
        x_slot = (x - my_x + n_x) % n_x
        return ((half * n_x + x_slot) * n_zh + zh) * local_rows + r

    built = build_descriptors(
        rows, position(pair_list[0]), position(pair_list[1]), pair_list[2]
    )

    product = jnp.dot(built, residuals, preferred_element_type=jnp.float32)
    widened = built.astype(jnp.float32)
    first_sums = jnp.sum(widened, axis=1)
    square_sums = jnp.sum(widened * widened, axis=1)
    col_part = jnp.sum(residuals.astype(jnp.float32), axis=0)
    local_samples = residuals.shape[0]

    local_means = first_sums / local_samples
    centred = product - local_means[:, None] * col_part[None, :]

    blocks = local_pairs // width_k
    block_rows = width_k + EXTRA_ROWS
    extras = jnp.concatenate(
        [
            split3(jnp.broadcast_to(col_part[None, :], (blocks, width_k))),
            split3(first_sums.reshape(blocks, width_k)),
            split3(square_sums.reshape(blocks, width_k)),
            jnp.zeros((blocks, EXTRA_ROWS - 9, width_k), jnp.bfloat16),
        ],
        axis=1,
    )
    packed = jnp.concatenate(
        [centred.astype(jnp.bfloat16).reshape(blocks, width_k, width_k), extras], axis=1
    )
    arrived = lax.all_to_all(packed, SAMP_AXES, 0, 0, tiled=False)
    centred_sum = jnp.sum(arrived[:, :width_k].astype(jnp.float32), axis=0)
    pieces = arrived[:, width_k:].astype(jnp.float32)

    def joined(i):
        return (pieces[:, i] + pieces[:, i + 1]) + pieces[:, i + 2]

    col_parts, first_parts, square_parts = joined(0), joined(3), joined(6)
    mean_share = jnp.einsum(
        "dp,dk->pk", first_parts / local_samples, col_parts,
        precision=lax.Precision.HIGHEST,
    )
    return finish(
        centred_sum + mean_share,
        jnp.sum(first_parts, axis=0),
        jnp.sum(square_parts, axis=0),
        jnp.sum(col_parts, axis=0),
        sample_count,
    )


def solution(mesh):
    n_feat, n_samp = mesh.devices.shape
    n_c, n_zh = 2, 2
    n_x = n_feat // (n_c * n_zh)
    n_zl = 4
    n_y = n_samp // n_zl
    devices = np.asarray(mesh.devices).reshape(n_x, n_zh, n_c, n_y, n_zl)
    fine = Mesh(devices, FEAT_AXES + SAMP_AXES)
    in_specs = (P(FEAT_AXES, SAMP_AXES), P(SAMP_AXES, None), P(None, FEAT_AXES))
    out_specs = P(FEAT_AXES + SAMP_AXES, None)
    return jax.shard_map(
        per_device, mesh=fine, in_specs=in_specs, out_specs=out_specs, check_vma=False
    )
```

```python
import math

import jax
import jax.numpy as jnp
from jax.experimental import pallas as pl
from jax.experimental.pallas import tpu as pltpu
import numpy as np
from jax import lax
from jax.sharding import Mesh
from jax.sharding import PartitionSpec as P

epsilon = 1e-05

FEAT_AXES = ("x", "zh", "c")
SAMP_AXES = ("y", "zl")
EXTRA_ROWS = 16
GATHER_TILE = 512


def combine_rows(first_rows, second_rows, operator_id):
    first_rows = first_rows.astype(jnp.float32)
    second_rows = second_rows.astype(jnp.float32)
    quotient = first_rows / (1.0 + jnp.abs(second_rows))
    built = jnp.where(
        operator_id == 0,
        first_rows + second_rows,
        jnp.where(
            operator_id == 1,
            first_rows - second_rows,
            jnp.where(operator_id == 2, first_rows * second_rows, quotient),
        ),
    )
    return built.astype(jnp.bfloat16)


def gather_kernel(first_ref, second_ref, table_ref, op_ref, out_ref, table, first_buf, second_buf):
    tile = first_buf.shape[0]
    step = 256

    @pl.when(pl.program_id(0) == 0)
    def _():
        def widen(i, carry):
            rows = pl.ds(pl.multiple_of(i * step, step), step)
            table[rows, :] = table_ref[rows, :].astype(jnp.float32)
            return carry
        lax.fori_loop(0, table.shape[0] // step, widen, 0)

    base = pl.program_id(0) * tile

    def body(g, carry):
        j0 = pl.multiple_of(g * 8, 8)
        firsts, seconds = [], []
        for t in range(8):
            firsts.append(table[pl.ds(first_ref[base + j0 + t], 1), :])
            seconds.append(table[pl.ds(second_ref[base + j0 + t], 1), :])
        first_buf[pl.ds(j0, 8), :] = jnp.concatenate(firsts, axis=0)
        second_buf[pl.ds(j0, 8), :] = jnp.concatenate(seconds, axis=0)
        return carry

    lax.fori_loop(0, tile // 8, body, 0, unroll=2)
    out_ref[...] = combine_rows(first_buf[...], second_buf[...], op_ref[...])


def build_descriptors(table, first_pos, second_pos, operator_id):
    n_rows, width = table.shape
    pairs = first_pos.shape[0]
    tile = min(GATHER_TILE, pairs)
    grid_spec = pltpu.PrefetchScalarGridSpec(
        num_scalar_prefetch=2,
        grid=(pairs // tile,),
        in_specs=[
            pl.BlockSpec((n_rows, width), lambda i, p1, p2: (0, 0)),
            pl.BlockSpec((tile, 1), lambda i, p1, p2: (i, 0)),
        ],
        out_specs=pl.BlockSpec((tile, width), lambda i, p1, p2: (i, 0)),
        scratch_shapes=[pltpu.VMEM((n_rows, width), jnp.float32)]
        + [pltpu.VMEM((tile, width), jnp.float32)] * 2,
    )
    return pl.pallas_call(
        gather_kernel,
        grid_spec=grid_spec,
        out_shape=jax.ShapeDtypeStruct((pairs, width), jnp.bfloat16),
        compiler_params=pltpu.CompilerParams(
            dimension_semantics=("arbitrary",), vmem_limit_bytes=60 * 1024 * 1024
        ),
        cost_estimate=pl.CostEstimate(
            flops=10 * pairs * width, transcendentals=0,
            bytes_accessed=n_rows * width * 2 + pairs * width * 2),
    )(first_pos, second_pos, table, operator_id[:, None])


def ring_gather(block, axis, n):
    assert n == 4
    fwd = [(i, (i + 1) % n) for i in range(n)]
    bwd = [(i, (i - 1) % n) for i in range(n)]
    from_left = lax.ppermute(block, axis, perm=fwd)
    from_right = lax.ppermute(block, axis, perm=bwd)
    half = block.shape[0] // 2
    far_a = lax.ppermute(from_left[:half], axis, perm=fwd)
    far_b = lax.ppermute(from_right[half:], axis, perm=bwd)
    return jnp.concatenate([block, from_right, far_a, far_b, from_left], axis=0)


def split3(v):
    hi = lax.reduce_precision(v, exponent_bits=8, mantissa_bits=7)
    rest = v - hi
    mid = lax.reduce_precision(rest, exponent_bits=8, mantissa_bits=7)
    lo = rest - mid
    return jnp.stack([hi, mid, lo], axis=-2).astype(jnp.bfloat16)


def finish(product, first_sums, square_sums, col_totals, sample_count):
    means = first_sums / sample_count
    variance = square_sums / sample_count - means * means
    centred = product - means[:, None] * col_totals[None, :]
    return centred * lax.rsqrt(variance + epsilon)[:, None] / math.sqrt(sample_count)


def per_device(tier_one, residuals, pair_list):
    local_rows = tier_one.shape[0]
    local_pairs = pair_list.shape[1]
    width_k = residuals.shape[1]
    n_x = lax.axis_size("x")
    n_zh = lax.axis_size("zh")
    n_y = lax.axis_size("y")
    n_zl = lax.axis_size("zl")
    n_samp = n_y * n_zl
    sample_count = residuals.shape[0] * n_samp

    rows = lax.all_gather(tier_one, "zh", axis=0, tiled=True)
    rows = ring_gather(rows, "x", n_x)
    other = lax.ppermute(rows, "c", perm=[(0, 1), (1, 0)])
    rows = jnp.concatenate([rows, other], axis=0)
    my_c = lax.axis_index("c")
    my_x = lax.axis_index("x")

    def position(g):
        f, r = g // local_rows, g % local_rows
        x, zh, c = f // (2 * n_zh), (f // 2) % n_zh, f % 2
        half = (c != my_c).astype(jnp.int32)
        x_slot = (x - my_x + n_x) % n_x
        return ((half * n_x + x_slot) * n_zh + zh) * local_rows + r

    built = build_descriptors(
        rows, position(pair_list[0]), position(pair_list[1]), pair_list[2]
    )

    product = jnp.dot(built, residuals, preferred_element_type=jnp.float32)
    widened = built.astype(jnp.float32)
    first_sums = jnp.sum(widened, axis=1)
    square_sums = jnp.sum(widened * widened, axis=1)
    col_part = jnp.sum(residuals.astype(jnp.float32), axis=0)
    local_samples = residuals.shape[0]

    local_means = first_sums / local_samples
    centred = product - local_means[:, None] * col_part[None, :]

    blocks = local_pairs // width_k
    block_rows = width_k + EXTRA_ROWS
    extras = jnp.concatenate(
        [
            split3(jnp.broadcast_to(col_part[None, :], (blocks, width_k))),
            split3(first_sums.reshape(blocks, width_k)),
            split3(square_sums.reshape(blocks, width_k)),
            jnp.zeros((blocks, EXTRA_ROWS - 9, width_k), jnp.bfloat16),
        ],
        axis=1,
    )
    packed = jnp.concatenate(
        [centred.astype(jnp.bfloat16).reshape(blocks, width_k, width_k), extras], axis=1
    )
    arrived = lax.all_to_all(packed, SAMP_AXES, 0, 0, tiled=False)
    centred_sum = jnp.sum(arrived[:, :width_k].astype(jnp.float32), axis=0)
    pieces = arrived[:, width_k:].astype(jnp.float32)

    def joined(i):
        return (pieces[:, i] + pieces[:, i + 1]) + pieces[:, i + 2]

    col_parts, first_parts, square_parts = joined(0), joined(3), joined(6)
    mean_share = jnp.einsum(
        "dp,dk->pk", first_parts / local_samples, col_parts,
        precision=lax.Precision.HIGHEST,
    )
    return finish(
        centred_sum + mean_share,
        jnp.sum(first_parts, axis=0),
        jnp.sum(square_parts, axis=0),
        jnp.sum(col_parts, axis=0),
        sample_count,
    )


def solution(mesh):
    n_feat, n_samp = mesh.devices.shape
    n_c, n_zh = 2, 2
    n_x = n_feat // (n_c * n_zh)
    n_zl = 4
    n_y = n_samp // n_zl
    devices = np.asarray(mesh.devices).reshape(n_x, n_zh, n_c, n_y, n_zl)
    fine = Mesh(devices, FEAT_AXES + SAMP_AXES)
    in_specs = (P(FEAT_AXES, SAMP_AXES), P(SAMP_AXES, None), P(None, FEAT_AXES))
    out_specs = P(FEAT_AXES + SAMP_AXES, None)
    return jax.shard_map(
        per_device, mesh=fine, in_specs=in_specs, out_specs=out_specs, check_vma=False
    )
```

```python
import math

import jax
import jax.numpy as jnp
from jax.experimental import pallas as pl
from jax.experimental.pallas import tpu as pltpu
import numpy as np
from jax import lax
from jax.sharding import Mesh
from jax.sharding import PartitionSpec as P

epsilon = 1e-05

FEAT_AXES = ("x", "zh", "c")
SAMP_AXES = ("y", "zl")
EXTRA_ROWS = 16
GATHER_TILE = 512


def combine_rows(first_rows, second_rows, operator_id):
    first_rows = first_rows.astype(jnp.float32)
    second_rows = second_rows.astype(jnp.float32)
    quotient = first_rows / (1.0 + jnp.abs(second_rows))
    built = jnp.where(
        operator_id == 0,
        first_rows + second_rows,
        jnp.where(
            operator_id == 1,
            first_rows - second_rows,
            jnp.where(operator_id == 2, first_rows * second_rows, quotient),
        ),
    )
    return built.astype(jnp.bfloat16)


def gather_kernel(first_ref, second_ref, own_ref, other_ref, op_ref, out_ref,
                  table, first_buf, second_buf):
    tile = first_buf.shape[0]
    step = 256
    half = own_ref.shape[0]

    @pl.when(pl.program_id(0) == 0)
    def _():
        def widen(i, carry):
            start = pl.multiple_of(i * step, step)
            table[pl.ds(start, step), :] = own_ref[pl.ds(start, step), :].astype(jnp.float32)
            table[pl.ds(start + half, step), :] = (
                other_ref[pl.ds(start, step), :].astype(jnp.float32))
            return carry
        lax.fori_loop(0, half // step, widen, 0)

    base = pl.program_id(0) * tile

    def body(g, carry):
        j0 = pl.multiple_of(g * 8, 8)
        firsts, seconds = [], []
        for t in range(8):
            firsts.append(table[pl.ds(first_ref[base + j0 + t], 1), :])
            seconds.append(table[pl.ds(second_ref[base + j0 + t], 1), :])
        first_buf[pl.ds(j0, 8), :] = jnp.concatenate(firsts, axis=0)
        second_buf[pl.ds(j0, 8), :] = jnp.concatenate(seconds, axis=0)
        return carry

    lax.fori_loop(0, tile // 8, body, 0)
    out_ref[...] = combine_rows(first_buf[...], second_buf[...], op_ref[...])


def build_descriptors(own, other, first_pos, second_pos, operator_id):
    half, width = own.shape
    n_rows = 2 * half
    pairs = first_pos.shape[0]
    tile = min(GATHER_TILE, pairs)
    grid_spec = pltpu.PrefetchScalarGridSpec(
        num_scalar_prefetch=2,
        grid=(pairs // tile,),
        in_specs=[
            pl.BlockSpec((half, width), lambda i, p1, p2: (0, 0)),
            pl.BlockSpec((half, width), lambda i, p1, p2: (0, 0)),
            pl.BlockSpec((tile, 1), lambda i, p1, p2: (i, 0)),
        ],
        out_specs=pl.BlockSpec((tile, width), lambda i, p1, p2: (i, 0)),
        scratch_shapes=[pltpu.VMEM((n_rows, width), jnp.float32)]
        + [pltpu.VMEM((tile, width), jnp.float32)] * 2,
    )
    return pl.pallas_call(
        gather_kernel,
        grid_spec=grid_spec,
        out_shape=jax.ShapeDtypeStruct((pairs, width), jnp.bfloat16),
        compiler_params=pltpu.CompilerParams(
            dimension_semantics=("arbitrary",), vmem_limit_bytes=60 * 1024 * 1024
        ),
        cost_estimate=pl.CostEstimate(
            flops=10 * pairs * width, transcendentals=0,
            bytes_accessed=n_rows * width * 2 + pairs * width * 2),
    )(first_pos, second_pos, own, other, operator_id[:, None])


def ring_gather(block, axis, n):
    assert n == 4
    fwd = [(i, (i + 1) % n) for i in range(n)]
    bwd = [(i, (i - 1) % n) for i in range(n)]
    from_left = lax.ppermute(block, axis, perm=fwd)
    from_right = lax.ppermute(block, axis, perm=bwd)
    half = block.shape[0] // 2
    far_a = lax.ppermute(from_left[:half], axis, perm=fwd)
    far_b = lax.ppermute(from_right[half:], axis, perm=bwd)
    return jnp.concatenate([block, from_right, far_a, far_b, from_left], axis=0)


def split3(v):
    hi = lax.reduce_precision(v, exponent_bits=8, mantissa_bits=7)
    rest = v - hi
    mid = lax.reduce_precision(rest, exponent_bits=8, mantissa_bits=7)
    lo = rest - mid
    return jnp.stack([hi, mid, lo], axis=-2).astype(jnp.bfloat16)


def finish(product, first_sums, square_sums, col_totals, sample_count):
    means = first_sums / sample_count
    variance = square_sums / sample_count - means * means
    centred = product - means[:, None] * col_totals[None, :]
    return centred * lax.rsqrt(variance + epsilon)[:, None] / math.sqrt(sample_count)


def per_device(tier_one, residuals, pair_list):
    local_rows = tier_one.shape[0]
    local_pairs = pair_list.shape[1]
    width_k = residuals.shape[1]
    n_x = lax.axis_size("x")
    n_zh = lax.axis_size("zh")
    n_y = lax.axis_size("y")
    n_zl = lax.axis_size("zl")
    n_samp = n_y * n_zl
    sample_count = residuals.shape[0] * n_samp

    rows = lax.all_gather(tier_one, "zh", axis=0, tiled=True)
    rows = ring_gather(rows, "x", n_x)
    other = lax.ppermute(rows, "c", perm=[(0, 1), (1, 0)])
    my_c = lax.axis_index("c")
    my_x = lax.axis_index("x")

    def position(g):
        f, r = g // local_rows, g % local_rows
        x, zh, c = f // (2 * n_zh), (f // 2) % n_zh, f % 2
        half = (c != my_c).astype(jnp.int32)
        x_slot = (x - my_x + n_x) % n_x
        return ((half * n_x + x_slot) * n_zh + zh) * local_rows + r

    built = build_descriptors(
        rows, other, position(pair_list[0]), position(pair_list[1]), pair_list[2]
    )

    product = jnp.dot(built, residuals, preferred_element_type=jnp.float32)
    widened = built.astype(jnp.float32)
    first_sums = jnp.sum(widened, axis=1)
    square_sums = jnp.sum(widened * widened, axis=1)
    col_part = jnp.sum(residuals.astype(jnp.float32), axis=0)
    local_samples = residuals.shape[0]

    local_means = first_sums / local_samples
    centred = product - local_means[:, None] * col_part[None, :]

    blocks = local_pairs // width_k
    block_rows = width_k + EXTRA_ROWS
    extras = jnp.concatenate(
        [
            split3(jnp.broadcast_to(col_part[None, :], (blocks, width_k))),
            split3(first_sums.reshape(blocks, width_k)),
            split3(square_sums.reshape(blocks, width_k)),
            jnp.zeros((blocks, EXTRA_ROWS - 9, width_k), jnp.bfloat16),
        ],
        axis=1,
    )
    packed = jnp.concatenate(
        [centred.astype(jnp.bfloat16).reshape(blocks, width_k, width_k), extras], axis=1
    )
    arrived = lax.all_to_all(packed, SAMP_AXES, 0, 0, tiled=False)
    centred_sum = jnp.sum(arrived[:, :width_k].astype(jnp.float32), axis=0)
    pieces = arrived[:, width_k:].astype(jnp.float32)

    def joined(i):
        return (pieces[:, i] + pieces[:, i + 1]) + pieces[:, i + 2]

    col_parts, first_parts, square_parts = joined(0), joined(3), joined(6)
    mean_share = jnp.einsum(
        "dp,dk->pk", first_parts / local_samples, col_parts,
        precision=lax.Precision.HIGHEST,
    )
    return finish(
        centred_sum + mean_share,
        jnp.sum(first_parts, axis=0),
        jnp.sum(square_parts, axis=0),
        jnp.sum(col_parts, axis=0),
        sample_count,
    )


def solution(mesh):
    n_feat, n_samp = mesh.devices.shape
    n_c, n_zh = 2, 2
    n_x = n_feat // (n_c * n_zh)
    n_zl = 4
    n_y = n_samp // n_zl
    devices = np.asarray(mesh.devices).reshape(n_x, n_zh, n_c, n_y, n_zl)
    fine = Mesh(devices, FEAT_AXES + SAMP_AXES)
    in_specs = (P(FEAT_AXES, SAMP_AXES), P(SAMP_AXES, None), P(None, FEAT_AXES))
    out_specs = P(FEAT_AXES + SAMP_AXES, None)
    return jax.shard_map(
        per_device, mesh=fine, in_specs=in_specs, out_specs=out_specs, check_vma=False
    )
```

```python
import math

import jax
import jax.numpy as jnp
from jax.experimental import pallas as pl
from jax.experimental.pallas import tpu as pltpu
import numpy as np
from jax import lax
from jax.sharding import Mesh
from jax.sharding import PartitionSpec as P

epsilon = 1e-05

FEAT_AXES = ("x", "zh", "c")
SAMP_AXES = ("y", "zl")
EXTRA_ROWS = 16
GATHER_TILE = 512


def combine_rows(first_rows, second_rows, operator_id):
    first_rows = first_rows.astype(jnp.float32)
    second_rows = second_rows.astype(jnp.float32)
    quotient = first_rows / (1.0 + jnp.abs(second_rows))
    built = jnp.where(
        operator_id == 0,
        first_rows + second_rows,
        jnp.where(
            operator_id == 1,
            first_rows - second_rows,
            jnp.where(operator_id == 2, first_rows * second_rows, quotient),
        ),
    )
    return built.astype(jnp.bfloat16)


def gather_kernel(first_ref, second_ref, own_ref, other_ref, op_ref, res_ref, col_ref,
                  centred_ref, first_ref_out, square_ref_out, table, first_buf, second_buf):
    tile = first_buf.shape[0]
    step = 256
    half = own_ref.shape[0]

    @pl.when(pl.program_id(0) == 0)
    def _():
        def widen(i, carry):
            start = pl.multiple_of(i * step, step)
            table[pl.ds(start, step), :] = own_ref[pl.ds(start, step), :].astype(jnp.float32)
            table[pl.ds(start + half, step), :] = (
                other_ref[pl.ds(start, step), :].astype(jnp.float32))
            return carry
        lax.fori_loop(0, half // step, widen, 0)

    base = pl.program_id(0) * tile

    def body(g, carry):
        j0 = pl.multiple_of(g * 8, 8)
        firsts, seconds = [], []
        for t in range(8):
            firsts.append(table[pl.ds(first_ref[base + j0 + t], 1), :])
            seconds.append(table[pl.ds(second_ref[base + j0 + t], 1), :])
        first_buf[pl.ds(j0, 8), :] = jnp.concatenate(firsts, axis=0)
        second_buf[pl.ds(j0, 8), :] = jnp.concatenate(seconds, axis=0)
        return carry

    lax.fori_loop(0, tile // 8, body, 0)
    built = combine_rows(first_buf[...], second_buf[...], op_ref[...])
    product = jnp.dot(built, res_ref[...], preferred_element_type=jnp.float32)
    widened = built.astype(jnp.float32)
    first_sums = jnp.sum(widened, axis=1, keepdims=True)
    first_ref_out[...] = first_sums
    square_ref_out[...] = jnp.sum(widened * widened, axis=1, keepdims=True)
    local_means = first_sums / res_ref.shape[0]
    centred_ref[...] = (product - local_means * col_ref[...]).astype(jnp.bfloat16)


def build_descriptors(own, other, first_pos, second_pos, operator_id, residuals, col_part):
    half, width = own.shape
    n_rows = 2 * half
    width_k = residuals.shape[1]
    pairs = first_pos.shape[0]
    tile = min(GATHER_TILE, pairs)
    grid_spec = pltpu.PrefetchScalarGridSpec(
        num_scalar_prefetch=2,
        grid=(pairs // tile,),
        in_specs=[
            pl.BlockSpec((half, width), lambda i, p1, p2: (0, 0)),
            pl.BlockSpec((half, width), lambda i, p1, p2: (0, 0)),
            pl.BlockSpec((tile, 1), lambda i, p1, p2: (i, 0)),
            pl.BlockSpec(residuals.shape, lambda i, p1, p2: (0, 0)),
            pl.BlockSpec((1, width_k), lambda i, p1, p2: (0, 0)),
        ],
        out_specs=[
            pl.BlockSpec((tile, width_k), lambda i, p1, p2: (i, 0)),
            pl.BlockSpec((tile, 1), lambda i, p1, p2: (i, 0)),
            pl.BlockSpec((tile, 1), lambda i, p1, p2: (i, 0)),
        ],
        scratch_shapes=[pltpu.VMEM((n_rows, width), jnp.float32)]
        + [pltpu.VMEM((tile, width), jnp.float32)] * 2,
    )
    return pl.pallas_call(
        gather_kernel,
        grid_spec=grid_spec,
        out_shape=[
            jax.ShapeDtypeStruct((pairs, width_k), jnp.bfloat16),
            jax.ShapeDtypeStruct((pairs, 1), jnp.float32),
            jax.ShapeDtypeStruct((pairs, 1), jnp.float32),
        ],
        compiler_params=pltpu.CompilerParams(
            dimension_semantics=("arbitrary",), vmem_limit_bytes=60 * 1024 * 1024
        ),
        cost_estimate=pl.CostEstimate(
            flops=(10 + 2 * width_k) * pairs * width, transcendentals=0,
            bytes_accessed=n_rows * width * 2 + pairs * width * 2),
    )(first_pos, second_pos, own, other, operator_id[:, None], residuals, col_part[None, :])


def ring_gather(block, axis, n):
    assert n == 4
    fwd = [(i, (i + 1) % n) for i in range(n)]
    bwd = [(i, (i - 1) % n) for i in range(n)]
    from_left = lax.ppermute(block, axis, perm=fwd)
    from_right = lax.ppermute(block, axis, perm=bwd)
    half = block.shape[0] // 2
    far_a = lax.ppermute(from_left[:half], axis, perm=fwd)
    far_b = lax.ppermute(from_right[half:], axis, perm=bwd)
    return jnp.concatenate([block, from_right, far_a, far_b, from_left], axis=0)


def split3(v):
    hi = lax.reduce_precision(v, exponent_bits=8, mantissa_bits=7)
    rest = v - hi
    mid = lax.reduce_precision(rest, exponent_bits=8, mantissa_bits=7)
    lo = rest - mid
    return jnp.stack([hi, mid, lo], axis=-2).astype(jnp.bfloat16)


def finish(product, first_sums, square_sums, col_totals, sample_count):
    means = first_sums / sample_count
    variance = square_sums / sample_count - means * means
    centred = product - means[:, None] * col_totals[None, :]
    return centred * lax.rsqrt(variance + epsilon)[:, None] / math.sqrt(sample_count)


def per_device(tier_one, residuals, pair_list):
    local_rows = tier_one.shape[0]
    local_pairs = pair_list.shape[1]
    width_k = residuals.shape[1]
    n_x = lax.axis_size("x")
    n_zh = lax.axis_size("zh")
    n_y = lax.axis_size("y")
    n_zl = lax.axis_size("zl")
    n_samp = n_y * n_zl
    sample_count = residuals.shape[0] * n_samp

    rows = lax.all_gather(tier_one, "zh", axis=0, tiled=True)
    rows = ring_gather(rows, "x", n_x)
    other = lax.ppermute(rows, "c", perm=[(0, 1), (1, 0)])
    my_c = lax.axis_index("c")
    my_x = lax.axis_index("x")

    def position(g):
        f, r = g // local_rows, g % local_rows
        x, zh, c = f // (2 * n_zh), (f // 2) % n_zh, f % 2
        half = (c != my_c).astype(jnp.int32)
        x_slot = (x - my_x + n_x) % n_x
        return ((half * n_x + x_slot) * n_zh + zh) * local_rows + r

    col_part = jnp.sum(residuals.astype(jnp.float32), axis=0)
    local_samples = residuals.shape[0]

    centred, first_sums, square_sums = build_descriptors(
        rows, other, position(pair_list[0]), position(pair_list[1]), pair_list[2],
        residuals, col_part,
    )

    blocks = local_pairs // width_k
    block_rows = width_k + EXTRA_ROWS
    extras = jnp.concatenate(
        [
            split3(jnp.broadcast_to(col_part[None, :], (blocks, width_k))),
            split3(first_sums.reshape(blocks, width_k)),
            split3(square_sums.reshape(blocks, width_k)),
            jnp.zeros((blocks, EXTRA_ROWS - 9, width_k), jnp.bfloat16),
        ],
        axis=1,
    )
    packed = jnp.concatenate(
        [centred.reshape(blocks, width_k, width_k), extras], axis=1
    )
    arrived = lax.all_to_all(packed, SAMP_AXES, 0, 0, tiled=False)
    centred_sum = jnp.sum(arrived[:, :width_k].astype(jnp.float32), axis=0)
    pieces = arrived[:, width_k:].astype(jnp.float32)

    def joined(i):
        return (pieces[:, i] + pieces[:, i + 1]) + pieces[:, i + 2]

    col_parts, first_parts, square_parts = joined(0), joined(3), joined(6)
    mean_share = jnp.einsum(
        "dp,dk->pk", first_parts / local_samples, col_parts,
        precision=lax.Precision.HIGHEST,
    )
    return finish(
        centred_sum + mean_share,
        jnp.sum(first_parts, axis=0),
        jnp.sum(square_parts, axis=0),
        jnp.sum(col_parts, axis=0),
        sample_count,
    )


def solution(mesh):
    n_feat, n_samp = mesh.devices.shape
    n_c, n_zh = 2, 2
    n_x = n_feat // (n_c * n_zh)
    n_zl = 4
    n_y = n_samp // n_zl
    devices = np.asarray(mesh.devices).reshape(n_x, n_zh, n_c, n_y, n_zl)
    fine = Mesh(devices, FEAT_AXES + SAMP_AXES)
    in_specs = (P(FEAT_AXES, SAMP_AXES), P(SAMP_AXES, None), P(None, FEAT_AXES))
    out_specs = P(FEAT_AXES + SAMP_AXES, None)
    return jax.shard_map(
        per_device, mesh=fine, in_specs=in_specs, out_specs=out_specs, check_vma=False
    )
```

```python
import math

import jax
import jax.numpy as jnp
from jax.experimental import pallas as pl
from jax.experimental.pallas import tpu as pltpu
import numpy as np
from jax import lax
from jax.sharding import Mesh
from jax.sharding import PartitionSpec as P

epsilon = 1e-05

FEAT_AXES = ("x", "zh", "c")
SAMP_AXES = ("y", "zl")
EXTRA_ROWS = 16
GATHER_TILE = 1024


def combine_rows(first_rows, second_rows, operator_id):
    first_rows = first_rows.astype(jnp.float32)
    second_rows = second_rows.astype(jnp.float32)
    quotient = first_rows / (1.0 + jnp.abs(second_rows))
    built = jnp.where(
        operator_id == 0,
        first_rows + second_rows,
        jnp.where(
            operator_id == 1,
            first_rows - second_rows,
            jnp.where(operator_id == 2, first_rows * second_rows, quotient),
        ),
    )
    return built.astype(jnp.bfloat16)


def gather_kernel(first_ref, second_ref, own_ref, other_ref, op_ref, out_ref,
                  table, first_buf, second_buf):
    tile = first_buf.shape[0]
    step = 256
    half = own_ref.shape[0]

    @pl.when(pl.program_id(0) == 0)
    def _():
        def widen(i, carry):
            start = pl.multiple_of(i * step, step)
            table[pl.ds(start, step), :] = own_ref[pl.ds(start, step), :].astype(jnp.float32)
            table[pl.ds(start + half, step), :] = (
                other_ref[pl.ds(start, step), :].astype(jnp.float32))
            return carry
        lax.fori_loop(0, half // step, widen, 0)

    base = pl.program_id(0) * tile

    def body(g, carry):
        j0 = pl.multiple_of(g * 8, 8)
        firsts, seconds = [], []
        for t in range(8):
            firsts.append(table[pl.ds(first_ref[base + j0 + t], 1), :])
            seconds.append(table[pl.ds(second_ref[base + j0 + t], 1), :])
        first_buf[pl.ds(j0, 8), :] = jnp.concatenate(firsts, axis=0)
        second_buf[pl.ds(j0, 8), :] = jnp.concatenate(seconds, axis=0)
        return carry

    lax.fori_loop(0, tile // 8, body, 0)
    out_ref[...] = combine_rows(first_buf[...], second_buf[...], op_ref[...])


def build_descriptors(own, other, first_pos, second_pos, operator_id):
    half, width = own.shape
    n_rows = 2 * half
    pairs = first_pos.shape[0]
    tile = min(GATHER_TILE, pairs)
    grid_spec = pltpu.PrefetchScalarGridSpec(
        num_scalar_prefetch=2,
        grid=(pairs // tile,),
        in_specs=[
            pl.BlockSpec((half, width), lambda i, p1, p2: (0, 0)),
            pl.BlockSpec((half, width), lambda i, p1, p2: (0, 0)),
            pl.BlockSpec((tile, 1), lambda i, p1, p2: (i, 0)),
        ],
        out_specs=pl.BlockSpec((tile, width), lambda i, p1, p2: (i, 0)),
        scratch_shapes=[pltpu.VMEM((n_rows, width), jnp.float32)]
        + [pltpu.VMEM((tile, width), jnp.float32)] * 2,
    )
    return pl.pallas_call(
        gather_kernel,
        grid_spec=grid_spec,
        out_shape=jax.ShapeDtypeStruct((pairs, width), jnp.bfloat16),
        compiler_params=pltpu.CompilerParams(
            dimension_semantics=("arbitrary",), vmem_limit_bytes=60 * 1024 * 1024
        ),
        cost_estimate=pl.CostEstimate(
            flops=10 * pairs * width, transcendentals=0,
            bytes_accessed=n_rows * width * 2 + pairs * width * 2),
    )(first_pos, second_pos, own, other, operator_id[:, None])


def ring_gather(block, axis, n):
    assert n == 4
    fwd = [(i, (i + 1) % n) for i in range(n)]
    bwd = [(i, (i - 1) % n) for i in range(n)]
    from_left = lax.ppermute(block, axis, perm=fwd)
    from_right = lax.ppermute(block, axis, perm=bwd)
    half = block.shape[0] // 2
    far_a = lax.ppermute(from_left[:half], axis, perm=fwd)
    far_b = lax.ppermute(from_right[half:], axis, perm=bwd)
    return jnp.concatenate([block, from_right, far_a, far_b, from_left], axis=0)


def split3(v):
    hi = lax.reduce_precision(v, exponent_bits=8, mantissa_bits=7)
    rest = v - hi
    mid = lax.reduce_precision(rest, exponent_bits=8, mantissa_bits=7)
    lo = rest - mid
    return jnp.stack([hi, mid, lo], axis=-2).astype(jnp.bfloat16)


def finish(product, first_sums, square_sums, col_totals, sample_count):
    means = first_sums / sample_count
    variance = square_sums / sample_count - means * means
    centred = product - means[:, None] * col_totals[None, :]
    return centred * lax.rsqrt(variance + epsilon)[:, None] / math.sqrt(sample_count)


def per_device(tier_one, residuals, pair_list):
    local_rows = tier_one.shape[0]
    local_pairs = pair_list.shape[1]
    width_k = residuals.shape[1]
    n_x = lax.axis_size("x")
    n_zh = lax.axis_size("zh")
    n_y = lax.axis_size("y")
    n_zl = lax.axis_size("zl")
    n_samp = n_y * n_zl
    sample_count = residuals.shape[0] * n_samp

    rows = lax.all_gather(tier_one, "zh", axis=0, tiled=True)
    rows = ring_gather(rows, "x", n_x)
    other = lax.ppermute(rows, "c", perm=[(0, 1), (1, 0)])
    my_c = lax.axis_index("c")
    my_x = lax.axis_index("x")

    def position(g):
        f, r = g // local_rows, g % local_rows
        x, zh, c = f // (2 * n_zh), (f // 2) % n_zh, f % 2
        half = (c != my_c).astype(jnp.int32)
        x_slot = (x - my_x + n_x) % n_x
        return ((half * n_x + x_slot) * n_zh + zh) * local_rows + r

    built = build_descriptors(
        rows, other, position(pair_list[0]), position(pair_list[1]), pair_list[2]
    )

    product = jnp.dot(built, residuals, preferred_element_type=jnp.float32)
    widened = built.astype(jnp.float32)
    first_sums = jnp.sum(widened, axis=1)
    square_sums = jnp.sum(widened * widened, axis=1)
    col_part = jnp.sum(residuals.astype(jnp.float32), axis=0)
    local_samples = residuals.shape[0]

    local_means = first_sums / local_samples
    centred = product - local_means[:, None] * col_part[None, :]

    blocks = local_pairs // width_k
    block_rows = width_k + EXTRA_ROWS
    extras = jnp.concatenate(
        [
            split3(jnp.broadcast_to(col_part[None, :], (blocks, width_k))),
            split3(first_sums.reshape(blocks, width_k)),
            split3(square_sums.reshape(blocks, width_k)),
            jnp.zeros((blocks, EXTRA_ROWS - 9, width_k), jnp.bfloat16),
        ],
        axis=1,
    )
    packed = jnp.concatenate(
        [centred.astype(jnp.bfloat16).reshape(blocks, width_k, width_k), extras], axis=1
    )
    arrived = lax.all_to_all(packed, SAMP_AXES, 0, 0, tiled=False)
    centred_sum = jnp.sum(arrived[:, :width_k].astype(jnp.float32), axis=0)
    pieces = arrived[:, width_k:].astype(jnp.float32)

    def joined(i):
        return (pieces[:, i] + pieces[:, i + 1]) + pieces[:, i + 2]

    col_parts, first_parts, square_parts = joined(0), joined(3), joined(6)
    mean_share = jnp.einsum(
        "dp,dk->pk", first_parts / local_samples, col_parts,
        precision=lax.Precision.HIGHEST,
    )
    return finish(
        centred_sum + mean_share,
        jnp.sum(first_parts, axis=0),
        jnp.sum(square_parts, axis=0),
        jnp.sum(col_parts, axis=0),
        sample_count,
    )


def solution(mesh):
    n_feat, n_samp = mesh.devices.shape
    n_c, n_zh = 2, 2
    n_x = n_feat // (n_c * n_zh)
    n_zl = 4
    n_y = n_samp // n_zl
    devices = np.asarray(mesh.devices).reshape(n_x, n_zh, n_c, n_y, n_zl)
    fine = Mesh(devices, FEAT_AXES + SAMP_AXES)
    in_specs = (P(FEAT_AXES, SAMP_AXES), P(SAMP_AXES, None), P(None, FEAT_AXES))
    out_specs = P(FEAT_AXES + SAMP_AXES, None)
    return jax.shard_map(
        per_device, mesh=fine, in_specs=in_specs, out_specs=out_specs, check_vma=False
    )
```

```python
import math

import jax
import jax.numpy as jnp
from jax.experimental import pallas as pl
from jax.experimental.pallas import tpu as pltpu
import numpy as np
from jax import lax
from jax.sharding import Mesh
from jax.sharding import PartitionSpec as P

epsilon = 1e-05

FEAT_AXES = ("x", "zh", "c")
SAMP_AXES = ("y", "zl")
EXTRA_ROWS = 16
GATHER_TILE = 512


def combine_rows(first_rows, second_rows, operator_id):
    first_rows = first_rows.astype(jnp.float32)
    second_rows = second_rows.astype(jnp.float32)
    quotient = first_rows / (1.0 + jnp.abs(second_rows))
    built = jnp.where(
        operator_id == 0,
        first_rows + second_rows,
        jnp.where(
            operator_id == 1,
            first_rows - second_rows,
            jnp.where(operator_id == 2, first_rows * second_rows, quotient),
        ),
    )
    return built.astype(jnp.bfloat16)


def gather_kernel(first_ref, second_ref, own_ref, other_ref, op_ref, out_ref,
                  table, first_buf, second_buf):
    tile = first_buf.shape[0]
    step = 256
    half = own_ref.shape[0]

    @pl.when(pl.program_id(0) == 0)
    def _():
        def widen(i, carry):
            start = pl.multiple_of(i * step, step)
            table[pl.ds(start, step), :] = own_ref[pl.ds(start, step), :].astype(jnp.float32)
            table[pl.ds(start + half, step), :] = (
                other_ref[pl.ds(start, step), :].astype(jnp.float32))
            return carry
        lax.fori_loop(0, half // step, widen, 0)

    base = pl.program_id(0) * tile

    def body(g, carry):
        j0 = pl.multiple_of(g * 8, 8)
        firsts, seconds = [], []
        for t in range(8):
            firsts.append(table[pl.ds(first_ref[base + j0 + t], 1), :])
            seconds.append(table[pl.ds(second_ref[base + j0 + t], 1), :])
        first_buf[pl.ds(j0, 8), :] = jnp.concatenate(firsts, axis=0)
        second_buf[pl.ds(j0, 8), :] = jnp.concatenate(seconds, axis=0)
        return carry

    lax.fori_loop(0, tile // 8, body, 0)
    out_ref[...] = combine_rows(first_buf[...], second_buf[...], op_ref[...])


def build_descriptors(own, other, first_pos, second_pos, operator_id):
    half, width = own.shape
    n_rows = 2 * half
    pairs = first_pos.shape[0]
    tile = min(GATHER_TILE, pairs)
    grid_spec = pltpu.PrefetchScalarGridSpec(
        num_scalar_prefetch=2,
        grid=(pairs // tile,),
        in_specs=[
            pl.BlockSpec((half, width), lambda i, p1, p2: (0, 0)),
            pl.BlockSpec((half, width), lambda i, p1, p2: (0, 0)),
            pl.BlockSpec((tile, 1), lambda i, p1, p2: (i, 0)),
        ],
        out_specs=pl.BlockSpec((tile, width), lambda i, p1, p2: (i, 0)),
        scratch_shapes=[pltpu.VMEM((n_rows, width), jnp.float32)]
        + [pltpu.VMEM((tile, width), jnp.float32)] * 2,
    )
    return pl.pallas_call(
        gather_kernel,
        grid_spec=grid_spec,
        out_shape=jax.ShapeDtypeStruct((pairs, width), jnp.bfloat16),
        compiler_params=pltpu.CompilerParams(
            dimension_semantics=("arbitrary",), vmem_limit_bytes=60 * 1024 * 1024
        ),
        cost_estimate=pl.CostEstimate(
            flops=10 * pairs * width, transcendentals=0,
            bytes_accessed=n_rows * width * 2 + pairs * width * 2),
    )(first_pos, second_pos, own, other, operator_id[:, None])


def ring_gather(block, axis, n):
    assert n == 4
    fwd = [(i, (i + 1) % n) for i in range(n)]
    bwd = [(i, (i - 1) % n) for i in range(n)]
    from_left = lax.ppermute(block, axis, perm=fwd)
    from_right = lax.ppermute(block, axis, perm=bwd)
    half = block.shape[0] // 2
    far_a = lax.ppermute(from_left[:half], axis, perm=fwd)
    far_b = lax.ppermute(from_right[half:], axis, perm=bwd)
    return jnp.concatenate([block, from_right, far_a, far_b, from_left], axis=0)


def split3(v):
    hi = lax.reduce_precision(v, exponent_bits=8, mantissa_bits=7)
    rest = v - hi
    mid = lax.reduce_precision(rest, exponent_bits=8, mantissa_bits=7)
    lo = rest - mid
    return jnp.stack([hi, mid, lo], axis=-2).astype(jnp.bfloat16)


def finish(product, first_sums, square_sums, col_totals, sample_count):
    means = first_sums / sample_count
    variance = square_sums / sample_count - means * means
    centred = product - means[:, None] * col_totals[None, :]
    return centred * lax.rsqrt(variance + epsilon)[:, None] / math.sqrt(sample_count)


def per_device(tier_one, residuals, pair_list):
    local_rows = tier_one.shape[0]
    local_pairs = pair_list.shape[1]
    width_k = residuals.shape[1]
    n_x = lax.axis_size("x")
    n_zh = lax.axis_size("zh")
    n_y = lax.axis_size("y")
    n_zl = lax.axis_size("zl")
    n_samp = n_y * n_zl
    sample_count = residuals.shape[0] * n_samp

    rows = lax.all_gather(tier_one, "zh", axis=0, tiled=True)
    rows = ring_gather(rows, "x", n_x)
    other = lax.ppermute(rows, "c", perm=[(0, 1), (1, 0)])
    my_c = lax.axis_index("c")
    my_x = lax.axis_index("x")

    def position(g):
        f, r = g // local_rows, g % local_rows
        x, zh, c = f // (2 * n_zh), (f // 2) % n_zh, f % 2
        half = (c != my_c).astype(jnp.int32)
        x_slot = (x - my_x + n_x) % n_x
        return ((half * n_x + x_slot) * n_zh + zh) * local_rows + r

    built = build_descriptors(
        rows, other, position(pair_list[0]), position(pair_list[1]), pair_list[2]
    )

    product = jnp.dot(built, residuals, preferred_element_type=jnp.float32)
    widened = built.astype(jnp.float32)
    first_sums = jnp.sum(widened, axis=1)
    square_sums = jnp.sum(widened * widened, axis=1)
    col_part = jnp.sum(residuals.astype(jnp.float32), axis=0)
    local_samples = residuals.shape[0]

    local_means = first_sums / local_samples
    centred = product - local_means[:, None] * col_part[None, :]

    blocks = local_pairs // width_k
    block_rows = width_k + EXTRA_ROWS
    extras = jnp.concatenate(
        [
            split3(jnp.broadcast_to(col_part[None, :], (blocks, width_k))),
            split3(first_sums.reshape(blocks, width_k)),
            split3(square_sums.reshape(blocks, width_k)),
            jnp.zeros((blocks, EXTRA_ROWS - 9, width_k), jnp.bfloat16),
        ],
        axis=1,
    )
    packed = jnp.concatenate(
        [centred.astype(jnp.bfloat16).reshape(blocks, width_k, width_k), extras], axis=1
    )
    by_zl = packed.reshape(n_y, n_zl, block_rows, width_k).transpose(1, 0, 2, 3)
    arrived = lax.all_to_all(
        by_zl.reshape(blocks, block_rows, width_k), ("zl", "y"), 0, 0, tiled=False
    )
    centred_sum = jnp.sum(arrived[:, :width_k].astype(jnp.float32), axis=0)
    pieces = arrived[:, width_k:].astype(jnp.float32)

    def joined(i):
        return (pieces[:, i] + pieces[:, i + 1]) + pieces[:, i + 2]

    col_parts, first_parts, square_parts = joined(0), joined(3), joined(6)
    mean_share = jnp.einsum(
        "dp,dk->pk", first_parts / local_samples, col_parts,
        precision=lax.Precision.HIGHEST,
    )
    return finish(
        centred_sum + mean_share,
        jnp.sum(first_parts, axis=0),
        jnp.sum(square_parts, axis=0),
        jnp.sum(col_parts, axis=0),
        sample_count,
    )


def solution(mesh):
    n_feat, n_samp = mesh.devices.shape
    n_c, n_zh = 2, 2
    n_x = n_feat // (n_c * n_zh)
    n_zl = 4
    n_y = n_samp // n_zl
    devices = np.asarray(mesh.devices).reshape(n_x, n_zh, n_c, n_y, n_zl)
    fine = Mesh(devices, FEAT_AXES + SAMP_AXES)
    in_specs = (P(FEAT_AXES, SAMP_AXES), P(SAMP_AXES, None), P(None, FEAT_AXES))
    out_specs = P(FEAT_AXES + SAMP_AXES, None)
    return jax.shard_map(
        per_device, mesh=fine, in_specs=in_specs, out_specs=out_specs, check_vma=False
    )
```

```python
import math

import jax
import jax.numpy as jnp
from jax.experimental import pallas as pl
from jax.experimental.pallas import tpu as pltpu
import numpy as np
from jax import lax
from jax.sharding import Mesh
from jax.sharding import PartitionSpec as P

epsilon = 1e-05

FEAT_AXES = ("x", "zh", "c")
SAMP_AXES = ("y", "zl")
EXTRA_ROWS = 16
GATHER_TILE = 512


def combine_rows(first_rows, second_rows, operator_id):
    first_rows = first_rows.astype(jnp.float32)
    second_rows = second_rows.astype(jnp.float32)
    quotient = first_rows / (1.0 + jnp.abs(second_rows))
    built = jnp.where(
        operator_id == 0,
        first_rows + second_rows,
        jnp.where(
            operator_id == 1,
            first_rows - second_rows,
            jnp.where(operator_id == 2, first_rows * second_rows, quotient),
        ),
    )
    return built.astype(jnp.bfloat16)


def gather_kernel(first_ref, second_ref, own_ref, near_ref, far_ref, op_ref, out_ref,
                  table, first_buf, second_buf):
    tile = first_buf.shape[0]
    step = 256

    @pl.when(pl.program_id(0) == 0)
    def _():
        offset = 0
        for piece in (own_ref, near_ref, far_ref):
            def widen(i, carry, piece=piece, offset=offset):
                start = pl.multiple_of(i * step, step)
                table[pl.ds(start + offset, step), :] = (
                    piece[pl.ds(start, step), :].astype(jnp.float32))
                return carry
            lax.fori_loop(0, piece.shape[0] // step, widen, 0)
            offset += piece.shape[0]

    base = pl.program_id(0) * tile

    def body(g, carry):
        j0 = pl.multiple_of(g * 8, 8)
        firsts, seconds = [], []
        for t in range(8):
            firsts.append(table[pl.ds(first_ref[base + j0 + t], 1), :])
            seconds.append(table[pl.ds(second_ref[base + j0 + t], 1), :])
        first_buf[pl.ds(j0, 8), :] = jnp.concatenate(firsts, axis=0)
        second_buf[pl.ds(j0, 8), :] = jnp.concatenate(seconds, axis=0)
        return carry

    lax.fori_loop(0, tile // 8, body, 0)
    out_ref[...] = combine_rows(first_buf[...], second_buf[...], op_ref[...])


def build_descriptors(own, near, far, first_pos, second_pos, operator_id):
    half, width = own.shape
    n_rows = half + near.shape[0] + far.shape[0]
    pairs = first_pos.shape[0]
    tile = min(GATHER_TILE, pairs)
    grid_spec = pltpu.PrefetchScalarGridSpec(
        num_scalar_prefetch=2,
        grid=(pairs // tile,),
        in_specs=[
            pl.BlockSpec(own.shape, lambda i, p1, p2: (0, 0)),
            pl.BlockSpec(near.shape, lambda i, p1, p2: (0, 0)),
            pl.BlockSpec(far.shape, lambda i, p1, p2: (0, 0)),
            pl.BlockSpec((tile, 1), lambda i, p1, p2: (i, 0)),
        ],
        out_specs=pl.BlockSpec((tile, width), lambda i, p1, p2: (i, 0)),
        scratch_shapes=[pltpu.VMEM((n_rows, width), jnp.float32)]
        + [pltpu.VMEM((tile, width), jnp.float32)] * 2,
    )
    return pl.pallas_call(
        gather_kernel,
        grid_spec=grid_spec,
        out_shape=jax.ShapeDtypeStruct((pairs, width), jnp.bfloat16),
        compiler_params=pltpu.CompilerParams(
            dimension_semantics=("arbitrary",), vmem_limit_bytes=60 * 1024 * 1024
        ),
        cost_estimate=pl.CostEstimate(
            flops=10 * pairs * width, transcendentals=0,
            bytes_accessed=n_rows * width * 2 + pairs * width * 2),
    )(first_pos, second_pos, own, near, far, operator_id[:, None])


def ring_gather(block, axis, n):
    assert n == 4
    fwd = [(i, (i + 1) % n) for i in range(n)]
    bwd = [(i, (i - 1) % n) for i in range(n)]
    from_left = lax.ppermute(block, axis, perm=fwd)
    from_right = lax.ppermute(block, axis, perm=bwd)
    half = block.shape[0] // 2
    far_a = lax.ppermute(from_left[:half], axis, perm=fwd)
    far_b = lax.ppermute(from_right[half:], axis, perm=bwd)
    return jnp.concatenate([block, from_right, far_a, far_b, from_left], axis=0)


def split3(v):
    hi = lax.reduce_precision(v, exponent_bits=8, mantissa_bits=7)
    rest = v - hi
    mid = lax.reduce_precision(rest, exponent_bits=8, mantissa_bits=7)
    lo = rest - mid
    return jnp.stack([hi, mid, lo], axis=-2).astype(jnp.bfloat16)


def finish(product, first_sums, square_sums, col_totals, sample_count):
    means = first_sums / sample_count
    variance = square_sums / sample_count - means * means
    centred = product - means[:, None] * col_totals[None, :]
    return centred * lax.rsqrt(variance + epsilon)[:, None] / math.sqrt(sample_count)


def per_device(tier_one, residuals, pair_list):
    local_rows = tier_one.shape[0]
    local_pairs = pair_list.shape[1]
    width_k = residuals.shape[1]
    n_x = lax.axis_size("x")
    n_zh = lax.axis_size("zh")
    n_y = lax.axis_size("y")
    n_zl = lax.axis_size("zl")
    n_samp = n_y * n_zl
    sample_count = residuals.shape[0] * n_samp

    pair_rows = lax.all_gather(tier_one, "zh", axis=0, tiled=True)
    swap = [(0, 1), (1, 0)]
    other_near = lax.ppermute(pair_rows, "c", perm=swap)
    rows = ring_gather(pair_rows, "x", n_x)
    other_far = lax.ppermute(rows[pair_rows.shape[0]:], "c", perm=swap)
    my_c = lax.axis_index("c")
    my_x = lax.axis_index("x")

    def position(g):
        f, r = g // local_rows, g % local_rows
        x, zh, c = f // (2 * n_zh), (f // 2) % n_zh, f % 2
        half = (c != my_c).astype(jnp.int32)
        x_slot = (x - my_x + n_x) % n_x
        return ((half * n_x + x_slot) * n_zh + zh) * local_rows + r

    built = build_descriptors(
        rows, other_near, other_far, position(pair_list[0]), position(pair_list[1]), pair_list[2]
    )

    product = jnp.dot(built, residuals, preferred_element_type=jnp.float32)
    widened = built.astype(jnp.float32)
    first_sums = jnp.sum(widened, axis=1)
    square_sums = jnp.sum(widened * widened, axis=1)
    col_part = jnp.sum(residuals.astype(jnp.float32), axis=0)
    local_samples = residuals.shape[0]

    local_means = first_sums / local_samples
    centred = product - local_means[:, None] * col_part[None, :]

    blocks = local_pairs // width_k
    block_rows = width_k + EXTRA_ROWS
    extras = jnp.concatenate(
        [
            split3(jnp.broadcast_to(col_part[None, :], (blocks, width_k))),
            split3(first_sums.reshape(blocks, width_k)),
            split3(square_sums.reshape(blocks, width_k)),
            jnp.zeros((blocks, EXTRA_ROWS - 9, width_k), jnp.bfloat16),
        ],
        axis=1,
    )
    packed = jnp.concatenate(
        [centred.astype(jnp.bfloat16).reshape(blocks, width_k, width_k), extras], axis=1
    )
    arrived = lax.all_to_all(packed, SAMP_AXES, 0, 0, tiled=False)
    centred_sum = jnp.sum(arrived[:, :width_k].astype(jnp.float32), axis=0)
    pieces = arrived[:, width_k:].astype(jnp.float32)

    def joined(i):
        return (pieces[:, i] + pieces[:, i + 1]) + pieces[:, i + 2]

    col_parts, first_parts, square_parts = joined(0), joined(3), joined(6)
    mean_share = jnp.einsum(
        "dp,dk->pk", first_parts / local_samples, col_parts,
        precision=lax.Precision.HIGHEST,
    )
    return finish(
        centred_sum + mean_share,
        jnp.sum(first_parts, axis=0),
        jnp.sum(square_parts, axis=0),
        jnp.sum(col_parts, axis=0),
        sample_count,
    )


def solution(mesh):
    n_feat, n_samp = mesh.devices.shape
    n_c, n_zh = 2, 2
    n_x = n_feat // (n_c * n_zh)
    n_zl = 4
    n_y = n_samp // n_zl
    devices = np.asarray(mesh.devices).reshape(n_x, n_zh, n_c, n_y, n_zl)
    fine = Mesh(devices, FEAT_AXES + SAMP_AXES)
    in_specs = (P(FEAT_AXES, SAMP_AXES), P(SAMP_AXES, None), P(None, FEAT_AXES))
    out_specs = P(FEAT_AXES + SAMP_AXES, None)
    return jax.shard_map(
        per_device, mesh=fine, in_specs=in_specs, out_specs=out_specs, check_vma=False
    )
```
